128 devices in a mesh: gx: 8 (over z, core), gy: 4 (over x), gz: 4 (over y).
Axes of the slice: x: 4, y: 4, z: 4, core: 2. Of those that a mesh axis runs over, the one named last changes fastest.
Arguments:
- residual_eq: float32 [3, 128, 128, 512], P(None, 'gx', 'gy', 'gz'), may hold values from -6 to 6
- diag_block: float32 [3, 3, 128, 128, 512], P(None, None, 'gx', 'gy', 'gz'), may hold values from -0.6 to 8, as said below
- mobility: float32 [3, 128, 128, 512], P(None, 'gx', 'gy', 'gz'), may hold values from 0.1 to 1
- trans: float32 [3, 128, 128, 512], P(None, 'gx', 'gy', 'gz'), may hold values from 3 to 3000
- perf_cell: int32 [65536], P(('gx', 'gy', 'gz')), may hold values from 0 to 65535
- perf_well: int32 [65536, 1], P(('gx', 'gy', 'gz')), may hold values from 0 to 2559, as said below
- perf_index: float32 [65536], P(('gx', 'gy', 'gz')), may hold values from 10 to 1000
Outputs:
- newton_update: float32 [3, 128, 128, 512], P(None, 'gx', 'gy', 'gz')
The draws below stay inside these ranges and needn't reach their ends.
Inputs may be any that keep to these rules, and one draw needn't show every extreme that they name: `diag_block`: in every 3 x 3 block the off-diagonal entries lie within -0.6 to 0.6 and the diagonal ones within 2 to 8. `perf_well`: every well has at least one perforation slot; all slots of well w lie on device number w // 20 or on the device after it along gz (number w // 20 + 1, same gx and gy).
All inputs are finite; a program needn't handle non-finite values.
Results may differ from the reference program's by a relative error of at most 0.0003.
Values sent between devices are 32-bit elements; how exact they have to be, the bound alone decides.
No kernel may reach another device: no remote copies, remote signals or barrier semaphores. Data moves between devices by JAX's collectives and lax.ppermute only.
A program may use at most 64 MiB of HBM per device.

```python
import math
import jax
import jax.numpy as jnp
from jax import lax

CX = 16
CY = 32
CZ = 128
WELL_DEV = 20
PERF_DEV = 512
CSWEEPS = 4
FSWEEPS = 6
NX = 128
NY = 128
NZ = 512
NWELLS = 2560
NPERF = 65536
N_GX = 8
N_GY = 4
N_GZ = 4
DEVICES = 128


def draw_diag_block(key, part):
    key_off, key_diag = jax.random.split(key)
    outside = jax.random.uniform(key_off, (3, 3, NX, NY, NZ), jnp.float32, -0.6, 0.6)
    spread = jax.random.uniform(key_diag, (3, NX, NY, NZ), jnp.float32, 0.0, 1.0)
    leading = 2.0 + 6.0 * spread
    identity = jnp.eye(3, dtype=jnp.float32)[:, :, None, None, None]
    return outside * (1.0 - identity) + identity * leading[:, None]


def draw_residual_eq(key, part):
    key_rough, key_phase = jax.random.split(key)
    phase = jax.random.uniform(key_phase, (3,), jnp.float32)
    along_x = jnp.cos(2.0 * math.pi * (jnp.arange(NX, dtype=jnp.float32) / NX + phase[0]))
    along_y = jnp.cos(2.0 * math.pi * (jnp.arange(NY, dtype=jnp.float32) / NY + phase[1]))
    along_z = jnp.cos(2.0 * math.pi * (jnp.arange(NZ, dtype=jnp.float32) / NZ + phase[2]))
    wave = along_x[:, None, None] * along_y[None, :, None] * along_z[None, None, :]
    mixing = jnp.array([1.0, 0.7, 0.5], jnp.float32)[:, None, None, None]
    rough = jnp.clip(jax.random.normal(key_rough, (3, NX, NY, NZ), jnp.float32), -4.0, 4.0)
    smooth = 0.9 * wave
    return rough + mixing * smooth[None]


def draw_trans(key, part):
    key_layer, key_cell = jax.random.split(key)
    layer_unit = jax.random.uniform(key_layer, (3, 1, 1, NZ), jnp.float32)
    cell_unit = jax.random.uniform(key_cell, (3, NX, NY, NZ), jnp.float32)
    layered = jnp.exp(math.log(100.0) * layer_unit)
    roughness = 0.3 * jnp.exp(math.log(10.0) * cell_unit)
    return 10.0 * layered * roughness


def perforations(key):
    base = jax.random.fold_in(key, 11)
    key_cut, key_end_x, key_end_y, key_slope_x, key_slope_y = jax.random.split(base, 5)
    runs = 2 * WELL_DEV
    scores = jax.random.randint(key_cut, (DEVICES, PERF_DEV - 1), 0, 1 << 20) * PERF_DEV + jnp.arange(1, PERF_DEV, dtype=jnp.int32)[None, :]
    best_scores, cut_slots = lax.top_k(scores, runs - 1)
    cuts = (cut_slots + 1).astype(jnp.int32)
    slots = jnp.arange(PERF_DEV, dtype=jnp.int32)
    starts = jnp.any(cuts[:, :, None] == slots[None, None, :], axis=1) | (slots == 0)[None, :]
    run = jnp.cumsum(starts.astype(jnp.int32), axis=1) - 1
    start_of = lax.cummax(jnp.where(starts, slots[None, :], 0), axis=1)
    next_mark = jnp.where(starts, slots[None, :], PERF_DEV)
    later = lax.cummin(next_mark, axis=1, reverse=True)
    next_start = jnp.concatenate([later[:, 1:], jnp.full((DEVICES, 1), PERF_DEV, jnp.int32)], axis=1)
    device = jnp.arange(DEVICES, dtype=jnp.int32)[:, None]
    layer = device % N_GZ
    upper = run < WELL_DEV
    owner = jnp.where(upper & (layer > 0), device - 1, device)
    well = (owner * WELL_DEV + jnp.where(upper, run, run - WELL_DEV)).astype(jnp.int32)
    offset = slots[None, :] - start_of
    depth = jnp.where(upper, jnp.where(layer > 0, CZ + offset, offset), CZ - next_start + slots[None, :])
    ends_x = jax.random.randint(key_end_x, (NWELLS,), 0, CX)
    ends_y = jax.random.randint(key_end_y, (NWELLS,), 0, CY)
    closing = jnp.arange(NWELLS, dtype=jnp.int32) % WELL_DEV == WELL_DEV - 1
    ends_x = jnp.where(closing, CX - 1, ends_x)
    ends_y = jnp.where(closing, CY - 1, ends_y)
    slope_x = jax.random.randint(key_slope_x, (NWELLS,), 0, 8)
    slope_y = jax.random.randint(key_slope_y, (NWELLS,), 0, 8)
    drift = depth - (CZ - 1)
    cell_x = (ends_x[well] + drift * slope_x[well] // 32) % CX
    cell_y = (ends_y[well] + drift * slope_y[well] // 32) % CY
    cell_z = depth % CZ
    cell = ((cell_x * CY + cell_y) * CZ + cell_z).astype(jnp.int32)
    return (cell.reshape(NPERF), well.reshape(NPERF, 1))


def draw_perf_cell(key, part):
    return perforations(key)[0]


def draw_perf_well(key, part):
    return perforations(key)[1]


def steps_of(stream_key, shape, cuts, low, largest):
    gain, own = 1.0, jax.random.fold_in(stream_key, 6)
    for dim, shards_of in cuts:
        steps = jnp.exp(jax.random.uniform(jax.random.fold_in(own, dim), (shards_of,), jnp.float32, low / len(cuts), largest / len(cuts)))
        gain = gain * jnp.repeat(steps, shape[dim] // shards_of).reshape([-1 if axis == dim else 1 for axis in range(len(shape))])
    return gain


def setup_inputs(seed: int = 0) -> dict:
    key_of = jax.random.split(jax.random.key(seed), 8)
    residual_eq = draw_residual_eq(jax.random.fold_in(key_of[7], 71), 0)
    diag_block = draw_diag_block(jax.random.fold_in(key_of[7], 71), 0)
    mobility = jnp.clip(jnp.exp(math.log(1.0) - 2.3025851 * jax.random.uniform(key_of[2], (3, NX, NY, NZ), jnp.float32) ** steps_of(key_of[2], (3, NX, NY, NZ), ((1, 8), (2, 4), (3, 4)), -0.2, 0.2)), 0.1, 1.0)
    trans = draw_trans(jax.random.fold_in(key_of[7], 71), 0)
    perf_cell = draw_perf_cell(jax.random.fold_in(key_of[7], 71), 0)
    perf_well = draw_perf_well(jax.random.fold_in(key_of[7], 71), 0)
    perf_index = jnp.clip(jnp.exp(math.log(1000.0) - 4.6051702 * jax.random.uniform(key_of[6], (NPERF,), jnp.float32) ** steps_of(key_of[6], (NPERF,), ((0, 128),), -0.2, 0.2)), 10.0, 1000.0)
    return dict(residual_eq=residual_eq, diag_block=diag_block, mobility=mobility, trans=trans, perf_cell=perf_cell, perf_well=perf_well, perf_index=perf_index)


omega_fine = 0.7
omega_coarse = 0.7

def block_solve(blocks, rhs):
    matrix = [[blocks[i, j] for j in range(3)] for i in range(3)]

    def cofactor(i, j):
        return matrix[(i + 1) % 3][(j + 1) % 3] * matrix[(i + 2) % 3][(j + 2) % 3] - matrix[(i + 1) % 3][(j + 2) % 3] * matrix[(i + 2) % 3][(j + 1) % 3]
    cofs = [[cofactor(i, j) for j in range(3)] for i in range(3)]
    determinant = matrix[0][0] * cofs[0][0] + matrix[0][1] * cofs[0][1] + matrix[0][2] * cofs[0][2]
    return jnp.stack([(cofs[0][j] * rhs[0] + cofs[1][j] * rhs[1] + cofs[2][j] * rhs[2]) / determinant for j in range(3)])

def face_flux(field, padded, trans, back):
    total = trans[0] * (field - padded[2:, 1:-1, 1:-1]) + back[0] * (field - padded[:-2, 1:-1, 1:-1])
    total = total + trans[1] * (field - padded[1:-1, 2:, 1:-1]) + back[1] * (field - padded[1:-1, :-2, 1:-1])
    total = total + trans[2] * (field - padded[1:-1, 1:-1, 2:]) + back[2] * (field - padded[1:-1, 1:-1, :-2])
    return total

def coarse_step(coarse, rhs_total, coefs, padded):
    dsum, plus_x, minus_x, plus_y, minus_y, plus_z, minus_z, cdiag = coefs
    applied = dsum * coarse + plus_x * (coarse - padded[2:, 1:-1, 1:-1]) + minus_x * (coarse - padded[:-2, 1:-1, 1:-1])
    applied = applied + plus_y * (coarse - padded[1:-1, 2:, 1:-1]) + minus_y * (coarse - padded[1:-1, :-2, 1:-1])
    applied = applied + plus_z * (coarse - padded[1:-1, 1:-1, 2:]) + minus_z * (coarse - padded[1:-1, 1:-1, :-2])
    return coarse + omega_coarse * (rhs_total - applied) / cdiag

def least_squares(beta, h11, h21, h12, h22, h32):
    r11 = jnp.sqrt(h11 * h11 + h21 * h21)
    cos_one = h11 / r11
    sin_one = h21 / r11
    g_first = cos_one * beta
    g_second = -sin_one * beta
    upper = cos_one * h12 + sin_one * h22
    lower = cos_one * h22 - sin_one * h12
    r22 = jnp.sqrt(lower * lower + h32 * h32)
    second = lower * g_second / (r22 * r22)
    first = (g_first - upper * second) / r11
    return (first, second)

def reference(residual_eq, diag_block, mobility, trans, perf_cell, perf_well, perf_index):
    zero_x = jnp.zeros((1, NY, NZ), jnp.float32)
    back = jnp.stack([jnp.concatenate([zero_x, trans[0, :-1]], 0), jnp.concatenate([jnp.zeros((NX, 1, NZ), jnp.float32), trans[1][:, :-1]], 1), jnp.concatenate([jnp.zeros((NX, NY, 1), jnp.float32), trans[2][:, :, :-1]], 2)])
    device = (jnp.arange(NPERF) // PERF_DEV).astype(jnp.int32)
    dev_x = device // (N_GY * N_GZ)
    dev_y = device // N_GZ % N_GY
    dev_z = device % N_GZ
    loc_x = perf_cell // (CY * CZ)
    loc_y = perf_cell // CZ % CY
    loc_z = perf_cell % CZ
    global_cell = (((dev_x * CX + loc_x) * NY + dev_y * CY + loc_y) * NZ + dev_z * CZ + loc_z).astype(jnp.int32)
    well_ids = perf_well[:, 0]
    weights = jax.ops.segment_sum(perf_index, well_ids, num_segments=NWELLS)

    def wells(field):
        values = field.reshape(-1)[global_cell]
        bottom = jax.ops.segment_sum(perf_index * values, well_ids, num_segments=NWELLS) / weights
        terms = perf_index * (values - bottom[well_ids])
        return jax.ops.segment_sum(terms, global_cell, num_segments=NX * NY * NZ).reshape(NX, NY, NZ)

    def flux(field):
        return face_flux(field, jnp.pad(field, 1), trans, back)

    def jacobian(vector):
        coupling = flux(vector[0]) + wells(vector[0])
        return diag_block[:, 0] * vector[0] + diag_block[:, 1] * vector[1] + diag_block[:, 2] * vector[2] + mobility * coupling[None]
    dpress = diag_block[0, 0] + diag_block[1, 0] + diag_block[2, 0]
    lam = mobility[0] + mobility[1] + mobility[2]
    pdiag = dpress + lam * (trans[0] + back[0] + trans[1] + back[1] + trans[2] + back[2])

    def blocked(field):
        return field.reshape(N_GX, CX, N_GY, CY, N_GZ, CZ)
    dsum = blocked(dpress).sum(axis=(1, 3, 5))
    plus_x = blocked(lam * trans[0])[:, -1].sum(axis=(2, 4))
    minus_x = blocked(lam * back[0])[:, 0].sum(axis=(2, 4))
    plus_y = blocked(lam * trans[1])[:, :, :, -1].sum(axis=(1, 4))
    minus_y = blocked(lam * back[1])[:, :, :, 0].sum(axis=(1, 4))
    plus_z = blocked(lam * trans[2])[:, :, :, :, :, -1].sum(axis=(1, 3))
    minus_z = blocked(lam * back[2])[:, :, :, :, :, 0].sum(axis=(1, 3))
    cdiag = dsum + plus_x + minus_x + plus_y + minus_y + plus_z + minus_z
    coefs = (dsum, plus_x, minus_x, plus_y, minus_y, plus_z, minus_z, cdiag)

    def precondition(vector):
        rpress = vector[0] + vector[1] + vector[2]
        rhs_total = blocked(rpress).sum(axis=(1, 3, 5))
        coarse = jnp.zeros((N_GX, N_GY, N_GZ), jnp.float32)
        for sweep in range(CSWEEPS):
            coarse = coarse_step(coarse, rhs_total, coefs, jnp.pad(coarse, 1))
        press = jnp.broadcast_to(coarse[:, None, :, None, :, None], (N_GX, CX, N_GY, CY, N_GZ, CZ)).reshape(NX, NY, NZ)
        for sweep in range(FSWEEPS):
            press = press + omega_fine * (rpress - (dpress * press + lam * flux(press))) / pdiag
        coupling = flux(press) + wells(press)
        applied = diag_block[:, 0] * press + mobility * coupling[None]
        correction = block_solve(diag_block, vector - applied)
        return jnp.concatenate([(correction[0] + press)[None], correction[1:]], 0)
    rhs = -residual_eq
    beta = jnp.sqrt(jnp.sum(rhs * rhs))
    first_basis = rhs / beta
    first_dir = precondition(first_basis)
    work = jacobian(first_dir)
    h11 = jnp.sum(first_basis * work)
    work = work - h11 * first_basis
    h21 = jnp.sqrt(jnp.sum(work * work))
    second_basis = work / h21
    second_dir = precondition(second_basis)
    work = jacobian(second_dir)
    h12 = jnp.sum(first_basis * work)
    h22 = jnp.sum(second_basis * work)
    work = work - h12 * first_basis
    work = work - h22 * second_basis
    h32 = jnp.sqrt(jnp.sum(work * work))
    first, second = least_squares(beta, h11, h21, h12, h22, h32)
    return first * first_dir + second * second_dir
```

```python
import jax
import jax.numpy as jnp
from jax import lax
from jax.sharding import PartitionSpec as P

WELL_DEV = 20
CSWEEPS = 4
FSWEEPS = 6


omega_fine = 0.7
omega_coarse = 0.7

AXES = ("gx", "gy", "gz")


def send_up(block, axis):
    size = lax.axis_size(axis)
    return lax.ppermute(block, axis, [(i, i + 1) for i in range(size - 1)])


def send_down(block, axis):
    size = lax.axis_size(axis)
    return lax.ppermute(block, axis, [(i + 1, i) for i in range(size - 1)])


def allsum(value):
    for axis in reversed(AXES):
        size = lax.axis_size(axis)
        if size & (size - 1):
            value = lax.psum(value, axis)
            continue
        step = 1
        while step < size:
            value = value + lax.ppermute(value, axis, [(i, i ^ step) for i in range(size)])
            step *= 2
    return value


def device_number():
    return (lax.axis_index("gx") * lax.axis_size("gy") + lax.axis_index("gy")) * lax.axis_size(
        "gz"
    ) + lax.axis_index("gz")


def gather_all(local):
    count = lax.axis_size("gx") * lax.axis_size("gy") * lax.axis_size("gz")
    slots = jnp.zeros((count, local.shape[0]), local.dtype).at[device_number()].set(local)
    return allsum(slots)


def block_solve(blocks, rhs):
    matrix = [[blocks[i, j] for j in range(3)] for i in range(3)]

    def cofactor(i, j):
        return (
            matrix[(i + 1) % 3][(j + 1) % 3] * matrix[(i + 2) % 3][(j + 2) % 3]
            - matrix[(i + 1) % 3][(j + 2) % 3] * matrix[(i + 2) % 3][(j + 1) % 3]
        )

    cofs = [[cofactor(i, j) for j in range(3)] for i in range(3)]
    determinant = matrix[0][0] * cofs[0][0] + matrix[0][1] * cofs[0][1] + matrix[0][2] * cofs[0][2]
    return jnp.stack(
        [
            (cofs[0][j] * rhs[0] + cofs[1][j] * rhs[1] + cofs[2][j] * rhs[2]) / determinant
            for j in range(3)
        ]
    )


def face_flux(field, faces, trans, back):
    x_next, x_prev, y_next, y_prev, z_next, z_prev = faces
    padded = jnp.pad(field, 1)
    padded = padded.at[-1:, 1:-1, 1:-1].set(x_next)
    padded = padded.at[:1, 1:-1, 1:-1].set(x_prev)
    padded = padded.at[1:-1, -1:, 1:-1].set(y_next)
    padded = padded.at[1:-1, :1, 1:-1].set(y_prev)
    padded = padded.at[1:-1, 1:-1, -1:].set(z_next)
    padded = padded.at[1:-1, 1:-1, :1].set(z_prev)
    total = trans[0] * (field - padded[2:, 1:-1, 1:-1]) + back[0] * (
        field - padded[:-2, 1:-1, 1:-1]
    )
    total = (
        total
        + trans[1] * (field - padded[1:-1, 2:, 1:-1])
        + back[1] * (field - padded[1:-1, :-2, 1:-1])
    )
    total = (
        total
        + trans[2] * (field - padded[1:-1, 1:-1, 2:])
        + back[2] * (field - padded[1:-1, 1:-1, :-2])
    )
    return total


def coarse_step(coarse, rhs_total, coefs, padded):
    dsum, plus_x, minus_x, plus_y, minus_y, plus_z, minus_z, cdiag = coefs
    applied = (
        dsum * coarse
        + plus_x * (coarse - padded[2:, 1:-1, 1:-1])
        + minus_x * (coarse - padded[:-2, 1:-1, 1:-1])
    )
    applied = (
        applied
        + plus_y * (coarse - padded[1:-1, 2:, 1:-1])
        + minus_y * (coarse - padded[1:-1, :-2, 1:-1])
    )
    applied = (
        applied
        + plus_z * (coarse - padded[1:-1, 1:-1, 2:])
        + minus_z * (coarse - padded[1:-1, 1:-1, :-2])
    )
    return coarse + omega_coarse * (rhs_total - applied) / cdiag


def least_squares(beta, h11, h21, h12, h22, h32):
    r11 = jnp.sqrt(h11 * h11 + h21 * h21)
    cos_one = h11 / r11
    sin_one = h21 / r11
    g_first = cos_one * beta
    g_second = -sin_one * beta
    upper = cos_one * h12 + sin_one * h22
    lower = cos_one * h22 - sin_one * h12
    r22 = jnp.sqrt(lower * lower + h32 * h32)
    second = lower * g_second / (r22 * r22)
    first = (g_first - upper * second) / r11
    return (first, second)


def shards(residual_eq, diag_block, mobility, trans, perf_cell, perf_well, perf_index):
    size_x = lax.axis_size("gx")
    size_y = lax.axis_size("gy")
    size_z = lax.axis_size("gz")
    cx, cy, cz = trans.shape[1:]
    ix = lax.axis_index("gx")
    iy = lax.axis_index("gy")
    iz = lax.axis_index("gz")

    local_well = perf_well[:, 0] - (device_number() - 1) * WELL_DEV

    def well_partials(values):
        return jax.ops.segment_sum(values, local_well, num_segments=2 * WELL_DEV)

    def exchange(field, partial):
        x_next = send_down(field[:1], "gx")
        x_prev = send_up(field[-1:], "gx")
        y_next = send_down(field[:, :1], "gy")
        y_prev = send_up(field[:, -1:], "gy")
        down = jnp.concatenate([field[:, :, 0].reshape(-1), partial[:WELL_DEV]])
        up = jnp.concatenate([field[:, :, -1].reshape(-1), partial[WELL_DEV:]])
        from_next = send_down(down, "gz")
        from_prev = send_up(up, "gz")
        z_next = from_next[: cx * cy].reshape(cx, cy, 1)
        z_prev = from_prev[: cx * cy].reshape(cx, cy, 1)
        totals = partial + jnp.concatenate([from_prev[cx * cy :], from_next[cx * cy :]])
        return (x_next, x_prev, y_next, y_prev, z_next, z_prev), totals

    weight_part = well_partials(perf_index)
    faces_t, weights = exchange(trans[2], weight_part)
    layer_x = send_up(trans[0, -1:], "gx")
    layer_y = send_up(trans[1][:, -1:], "gy")
    layer_z = faces_t[5]
    back = jnp.stack(
        [
            jnp.concatenate([layer_x, trans[0, :-1]], 0),
            jnp.concatenate([layer_y, trans[1][:, :-1]], 1),
            jnp.concatenate([layer_z, trans[2][:, :, :-1]], 2),
        ]
    )

    def flux(field, faces):
        return face_flux(field, faces, trans, back)

    def flux_wells(field):
        flat = field.reshape(-1)
        values = flat[perf_cell]
        faces, totals = exchange(field, well_partials(perf_index * values))
        bottom = (totals / weights)[local_well]
        terms = perf_index * (values - bottom)
        wells = jnp.zeros_like(flat).at[perf_cell].add(terms).reshape(field.shape)
        return flux(field, faces) + wells

    def jacobian(vector):
        coupling = flux_wells(vector[0])
        return (
            diag_block[:, 0] * vector[0]
            + diag_block[:, 1] * vector[1]
            + diag_block[:, 2] * vector[2]
            + mobility * coupling[None]
        )

    dpress = diag_block[0, 0] + diag_block[1, 0] + diag_block[2, 0]
    lam = mobility[0] + mobility[1] + mobility[2]
    pdiag = dpress + lam * (trans[0] + back[0] + trans[1] + back[1] + trans[2] + back[2])
    dsum = jnp.sum(dpress)
    plus_x = jnp.sum(lam[-1] * trans[0, -1])
    minus_x = jnp.sum(lam[0] * back[0, 0])
    plus_y = jnp.sum(lam[:, -1] * trans[1][:, -1])
    minus_y = jnp.sum(lam[:, 0] * back[1][:, 0])
    plus_z = jnp.sum(lam[:, :, -1] * trans[2][:, :, -1])
    minus_z = jnp.sum(lam[:, :, 0] * back[2][:, :, 0])

    rhs = -residual_eq
    start = gather_all(
        jnp.stack(
            [
                jnp.sum(rhs * rhs),
                jnp.sum(rhs[0] + rhs[1] + rhs[2]),
                dsum,
                plus_x,
                minus_x,
                plus_y,
                minus_y,
                plus_z,
                minus_z,
            ]
        )
    )
    grid = (size_x, size_y, size_z)
    beta = jnp.sqrt(jnp.sum(start[:, 0]))
    coarse_coefs = [start[:, k].reshape(grid) for k in range(2, 9)]
    cdiag = coarse_coefs[0]
    for value in coarse_coefs[1:]:
        cdiag = cdiag + value
    coarse_coefs = tuple(coarse_coefs) + (cdiag,)

    def coarse_solve(rhs_total):
        coarse = jnp.zeros(grid, jnp.float32)
        for sweep in range(CSWEEPS):
            coarse = coarse_step(coarse, rhs_total, coarse_coefs, jnp.pad(coarse, 1))
        padded = jnp.pad(coarse, 1)

        def at(dx, dy, dz):
            return padded[ix + 1 + dx, iy + 1 + dy, iz + 1 + dz]

        faces = (
            jnp.broadcast_to(at(1, 0, 0), (1, cy, cz)),
            jnp.broadcast_to(at(-1, 0, 0), (1, cy, cz)),
            jnp.broadcast_to(at(0, 1, 0), (cx, 1, cz)),
            jnp.broadcast_to(at(0, -1, 0), (cx, 1, cz)),
            jnp.broadcast_to(at(0, 0, 1), (cx, cy, 1)),
            jnp.broadcast_to(at(0, 0, -1), (cx, cy, 1)),
        )
        return at(0, 0, 0), faces

    def precondition(vector, rhs_total):
        rpress = vector[0] + vector[1] + vector[2]
        own, faces = coarse_solve(rhs_total)
        press = jnp.broadcast_to(own, rpress.shape)
        for sweep in range(FSWEEPS):
            if sweep:
                faces, _ = exchange(press, jnp.zeros((2 * WELL_DEV,), jnp.float32))
            press = press + omega_fine * (rpress - (dpress * press + lam * flux(press, faces))) / pdiag
        coupling = flux_wells(press)
        applied = diag_block[:, 0] * press + mobility * coupling[None]
        correction = block_solve(diag_block, vector - applied)
        return jnp.concatenate([(correction[0] + press)[None], correction[1:]], 0)

    first_basis = rhs / beta
    first_dir = precondition(first_basis, start[:, 1].reshape(grid) / beta)
    work = jacobian(first_dir)
    h11 = allsum(jnp.sum(first_basis * work))
    work = work - h11 * first_basis
    second = gather_all(jnp.stack([jnp.sum(work * work), jnp.sum(work[0] + work[1] + work[2])]))
    h21 = jnp.sqrt(jnp.sum(second[:, 0]))
    second_basis = work / h21
    second_dir = precondition(second_basis, second[:, 1].reshape(grid) / h21)
    work = jacobian(second_dir)
    products = allsum(jnp.stack([jnp.sum(first_basis * work), jnp.sum(second_basis * work)]))
    h12 = products[0]
    h22 = products[1]
    work = work - h12 * first_basis
    work = work - h22 * second_basis
    h32 = jnp.sqrt(allsum(jnp.sum(work * work)))
    first, second = least_squares(beta, h11, h21, h12, h22, h32)
    return first * first_dir + second * second_dir


def solution(mesh):
    in_specs = (
        P(None, "gx", "gy", "gz"),
        P(None, None, "gx", "gy", "gz"),
        P(None, "gx", "gy", "gz"),
        P(None, "gx", "gy", "gz"),
        P(("gx", "gy", "gz")),
        P(("gx", "gy", "gz"), None),
        P(("gx", "gy", "gz")),
    )
    out_specs = P(None, "gx", "gy", "gz")
    return jax.shard_map(shards, mesh=mesh, in_specs=in_specs, out_specs=out_specs, check_vma=False)
```

```python
import jax
import jax.numpy as jnp
from jax import lax
from jax.sharding import PartitionSpec as P

WELL_DEV = 20
CSWEEPS = 4
FSWEEPS = 6


omega_fine = 0.7
omega_coarse = 0.7

AXES = ("gx", "gy", "gz")


def send_up(block, axis):
    size = lax.axis_size(axis)
    return lax.ppermute(block, axis, [(i, i + 1) for i in range(size - 1)])


def send_down(block, axis):
    size = lax.axis_size(axis)
    return lax.ppermute(block, axis, [(i + 1, i) for i in range(size - 1)])


def allsum(value):
    for axis in reversed(AXES):
        size = lax.axis_size(axis)
        if size & (size - 1):
            value = lax.psum(value, axis)
            continue
        step = 1
        while step < size:
            value = value + lax.ppermute(value, axis, [(i, i ^ step) for i in range(size)])
            step *= 2
    return value


def device_number():
    return (lax.axis_index("gx") * lax.axis_size("gy") + lax.axis_index("gy")) * lax.axis_size(
        "gz"
    ) + lax.axis_index("gz")


def gather_all(local):
    count = lax.axis_size("gx") * lax.axis_size("gy") * lax.axis_size("gz")
    slots = jnp.zeros((count, local.shape[0]), local.dtype).at[device_number()].set(local)
    return allsum(slots)


def block_solve(blocks, rhs):
    matrix = [[blocks[i, j] for j in range(3)] for i in range(3)]

    def cofactor(i, j):
        return (
            matrix[(i + 1) % 3][(j + 1) % 3] * matrix[(i + 2) % 3][(j + 2) % 3]
            - matrix[(i + 1) % 3][(j + 2) % 3] * matrix[(i + 2) % 3][(j + 1) % 3]
        )

    cofs = [[cofactor(i, j) for j in range(3)] for i in range(3)]
    determinant = matrix[0][0] * cofs[0][0] + matrix[0][1] * cofs[0][1] + matrix[0][2] * cofs[0][2]
    return jnp.stack(
        [
            (cofs[0][j] * rhs[0] + cofs[1][j] * rhs[1] + cofs[2][j] * rhs[2]) / determinant
            for j in range(3)
        ]
    )


def face_flux(field, faces, trans, back):
    x_next, x_prev, y_next, y_prev, z_next, z_prev = faces
    padded = jnp.concatenate([x_prev, field, x_next], 0)
    rim_x = ((1, 1), (0, 0), (0, 0))
    padded = jnp.concatenate([jnp.pad(y_prev, rim_x), padded, jnp.pad(y_next, rim_x)], 1)
    rim_xy = ((1, 1), (1, 1), (0, 0))
    padded = jnp.concatenate([jnp.pad(z_prev, rim_xy), padded, jnp.pad(z_next, rim_xy)], 2)
    total = trans[0] * (field - padded[2:, 1:-1, 1:-1]) + back[0] * (
        field - padded[:-2, 1:-1, 1:-1]
    )
    total = (
        total
        + trans[1] * (field - padded[1:-1, 2:, 1:-1])
        + back[1] * (field - padded[1:-1, :-2, 1:-1])
    )
    total = (
        total
        + trans[2] * (field - padded[1:-1, 1:-1, 2:])
        + back[2] * (field - padded[1:-1, 1:-1, :-2])
    )
    return total


def coarse_step(coarse, rhs_total, coefs, padded):
    dsum, plus_x, minus_x, plus_y, minus_y, plus_z, minus_z, cdiag = coefs
    applied = (
        dsum * coarse
        + plus_x * (coarse - padded[2:, 1:-1, 1:-1])
        + minus_x * (coarse - padded[:-2, 1:-1, 1:-1])
    )
    applied = (
        applied
        + plus_y * (coarse - padded[1:-1, 2:, 1:-1])
        + minus_y * (coarse - padded[1:-1, :-2, 1:-1])
    )
    applied = (
        applied
        + plus_z * (coarse - padded[1:-1, 1:-1, 2:])
        + minus_z * (coarse - padded[1:-1, 1:-1, :-2])
    )
    return coarse + omega_coarse * (rhs_total - applied) / cdiag


def least_squares(beta, h11, h21, h12, h22, h32):
    r11 = jnp.sqrt(h11 * h11 + h21 * h21)
    cos_one = h11 / r11
    sin_one = h21 / r11
    g_first = cos_one * beta
    g_second = -sin_one * beta
    upper = cos_one * h12 + sin_one * h22
    lower = cos_one * h22 - sin_one * h12
    r22 = jnp.sqrt(lower * lower + h32 * h32)
    second = lower * g_second / (r22 * r22)
    first = (g_first - upper * second) / r11
    return (first, second)


def shards(residual_eq, diag_block, mobility, trans, perf_cell, perf_well, perf_index):
    size_x = lax.axis_size("gx")
    size_y = lax.axis_size("gy")
    size_z = lax.axis_size("gz")
    cx, cy, cz = trans.shape[1:]
    ix = lax.axis_index("gx")
    iy = lax.axis_index("gy")
    iz = lax.axis_index("gz")

    local_well = perf_well[:, 0] - (device_number() - 1) * WELL_DEV

    slot_of_well = local_well[:, None] == jnp.arange(2 * WELL_DEV, dtype=local_well.dtype)[None, :]

    def well_partials(values):
        return jnp.sum(jnp.where(slot_of_well, values[:, None], 0.0), axis=0)

    def per_slot(table):
        return jnp.sum(jnp.where(slot_of_well, table[None, :], 0.0), axis=1)

    def exchange(field, partial):
        x_next = send_down(field[:1], "gx")
        x_prev = send_up(field[-1:], "gx")
        y_next = send_down(field[:, :1], "gy")
        y_prev = send_up(field[:, -1:], "gy")
        down = jnp.concatenate([field[:, :, 0].reshape(-1), partial[:WELL_DEV]])
        up = jnp.concatenate([field[:, :, -1].reshape(-1), partial[WELL_DEV:]])
        from_next = send_down(down, "gz")
        from_prev = send_up(up, "gz")
        z_next = from_next[: cx * cy].reshape(cx, cy, 1)
        z_prev = from_prev[: cx * cy].reshape(cx, cy, 1)
        totals = partial + jnp.concatenate([from_prev[cx * cy :], from_next[cx * cy :]])
        return (x_next, x_prev, y_next, y_prev, z_next, z_prev), totals

    weight_part = well_partials(perf_index)
    faces_t, weights = exchange(trans[2], weight_part)
    layer_x = send_up(trans[0, -1:], "gx")
    layer_y = send_up(trans[1][:, -1:], "gy")
    layer_z = faces_t[5]
    back = jnp.stack(
        [
            jnp.concatenate([layer_x, trans[0, :-1]], 0),
            jnp.concatenate([layer_y, trans[1][:, :-1]], 1),
            jnp.concatenate([layer_z, trans[2][:, :, :-1]], 2),
        ]
    )

    def flux(field, faces):
        return face_flux(field, faces, trans, back)

    def flux_wells(field):
        flat = field.reshape(-1)
        values = flat[perf_cell]
        faces, totals = exchange(field, well_partials(perf_index * values))
        bottom = per_slot(totals / weights)
        terms = perf_index * (values - bottom)
        wells = jnp.zeros_like(flat).at[perf_cell].add(terms).reshape(field.shape)
        return flux(field, faces) + wells

    def jacobian(vector):
        coupling = flux_wells(vector[0])
        return (
            diag_block[:, 0] * vector[0]
            + diag_block[:, 1] * vector[1]
            + diag_block[:, 2] * vector[2]
            + mobility * coupling[None]
        )

    dpress = diag_block[0, 0] + diag_block[1, 0] + diag_block[2, 0]
    lam = mobility[0] + mobility[1] + mobility[2]
    pdiag = dpress + lam * (trans[0] + back[0] + trans[1] + back[1] + trans[2] + back[2])
    dsum = jnp.sum(dpress)
    plus_x = jnp.sum(lam[-1] * trans[0, -1])
    minus_x = jnp.sum(lam[0] * back[0, 0])
    plus_y = jnp.sum(lam[:, -1] * trans[1][:, -1])
    minus_y = jnp.sum(lam[:, 0] * back[1][:, 0])
    plus_z = jnp.sum(lam[:, :, -1] * trans[2][:, :, -1])
    minus_z = jnp.sum(lam[:, :, 0] * back[2][:, :, 0])

    rhs = -residual_eq
    start = gather_all(
        jnp.stack(
            [
                jnp.sum(rhs * rhs),
                jnp.sum(rhs[0] + rhs[1] + rhs[2]),
                dsum,
                plus_x,
                minus_x,
                plus_y,
                minus_y,
                plus_z,
                minus_z,
            ]
        )
    )
    grid = (size_x, size_y, size_z)
    beta = jnp.sqrt(jnp.sum(start[:, 0]))
    coarse_coefs = [start[:, k].reshape(grid) for k in range(2, 9)]
    cdiag = coarse_coefs[0]
    for value in coarse_coefs[1:]:
        cdiag = cdiag + value
    coarse_coefs = tuple(coarse_coefs) + (cdiag,)

    def coarse_solve(rhs_total):
        coarse = jnp.zeros(grid, jnp.float32)
        for sweep in range(CSWEEPS):
            coarse = coarse_step(coarse, rhs_total, coarse_coefs, jnp.pad(coarse, 1))
        padded = jnp.pad(coarse, 1)

        def at(dx, dy, dz):
            return padded[ix + 1 + dx, iy + 1 + dy, iz + 1 + dz]

        faces = (
            jnp.broadcast_to(at(1, 0, 0), (1, cy, cz)),
            jnp.broadcast_to(at(-1, 0, 0), (1, cy, cz)),
            jnp.broadcast_to(at(0, 1, 0), (cx, 1, cz)),
            jnp.broadcast_to(at(0, -1, 0), (cx, 1, cz)),
            jnp.broadcast_to(at(0, 0, 1), (cx, cy, 1)),
            jnp.broadcast_to(at(0, 0, -1), (cx, cy, 1)),
        )
        return at(0, 0, 0), faces

    def precondition(vector, rhs_total):
        rpress = vector[0] + vector[1] + vector[2]
        own, faces = coarse_solve(rhs_total)
        press = jnp.broadcast_to(own, rpress.shape)
        for sweep in range(FSWEEPS):
            if sweep:
                faces, _ = exchange(press, jnp.zeros((2 * WELL_DEV,), jnp.float32))
            press = press + omega_fine * (rpress - (dpress * press + lam * flux(press, faces))) / pdiag
        coupling = flux_wells(press)
        applied = diag_block[:, 0] * press + mobility * coupling[None]
        correction = block_solve(diag_block, vector - applied)
        return jnp.concatenate([(correction[0] + press)[None], correction[1:]], 0)

    first_basis = rhs / beta
    first_dir = precondition(first_basis, start[:, 1].reshape(grid) / beta)
    work = jacobian(first_dir)
    h11 = allsum(jnp.sum(first_basis * work))
    work = work - h11 * first_basis
    second = gather_all(jnp.stack([jnp.sum(work * work), jnp.sum(work[0] + work[1] + work[2])]))
    h21 = jnp.sqrt(jnp.sum(second[:, 0]))
    second_basis = work / h21
    second_dir = precondition(second_basis, second[:, 1].reshape(grid) / h21)
    work = jacobian(second_dir)
    products = allsum(jnp.stack([jnp.sum(first_basis * work), jnp.sum(second_basis * work)]))
    h12 = products[0]
    h22 = products[1]
    work = work - h12 * first_basis
    work = work - h22 * second_basis
    h32 = jnp.sqrt(allsum(jnp.sum(work * work)))
    first, second = least_squares(beta, h11, h21, h12, h22, h32)
    return first * first_dir + second * second_dir


def solution(mesh):
    in_specs = (
        P(None, "gx", "gy", "gz"),
        P(None, None, "gx", "gy", "gz"),
        P(None, "gx", "gy", "gz"),
        P(None, "gx", "gy", "gz"),
        P(("gx", "gy", "gz")),
        P(("gx", "gy", "gz"), None),
        P(("gx", "gy", "gz")),
    )
    out_specs = P(None, "gx", "gy", "gz")
    return jax.shard_map(shards, mesh=mesh, in_specs=in_specs, out_specs=out_specs, check_vma=False)
```

```python
import jax
import jax.numpy as jnp
from jax import lax
from jax.sharding import PartitionSpec as P

WELL_DEV = 20
CSWEEPS = 4
FSWEEPS = 6


omega_fine = 0.7
omega_coarse = 0.7

AXES = ("gx", "gy", "gz")


def send_up(block, axis):
    size = lax.axis_size(axis)
    return lax.ppermute(block, axis, [(i, i + 1) for i in range(size - 1)])


def send_down(block, axis):
    size = lax.axis_size(axis)
    return lax.ppermute(block, axis, [(i + 1, i) for i in range(size - 1)])


def allsum(value):
    for axis in reversed(AXES):
        size = lax.axis_size(axis)
        if size & (size - 1):
            value = lax.psum(value, axis)
            continue
        step = 1
        while step < size:
            value = value + lax.ppermute(value, axis, [(i, i ^ step) for i in range(size)])
            step *= 2
    return value


def device_number():
    return (lax.axis_index("gx") * lax.axis_size("gy") + lax.axis_index("gy")) * lax.axis_size(
        "gz"
    ) + lax.axis_index("gz")


def gather_all(local):
    count = lax.axis_size("gx") * lax.axis_size("gy") * lax.axis_size("gz")
    slots = jnp.zeros((count, local.shape[0]), local.dtype).at[device_number()].set(local)
    return allsum(slots)


def block_solve(blocks, rhs):
    matrix = [[blocks[i, j] for j in range(3)] for i in range(3)]

    def cofactor(i, j):
        return (
            matrix[(i + 1) % 3][(j + 1) % 3] * matrix[(i + 2) % 3][(j + 2) % 3]
            - matrix[(i + 1) % 3][(j + 2) % 3] * matrix[(i + 2) % 3][(j + 1) % 3]
        )

    cofs = [[cofactor(i, j) for j in range(3)] for i in range(3)]
    determinant = matrix[0][0] * cofs[0][0] + matrix[0][1] * cofs[0][1] + matrix[0][2] * cofs[0][2]
    return jnp.stack(
        [
            (cofs[0][j] * rhs[0] + cofs[1][j] * rhs[1] + cofs[2][j] * rhs[2]) / determinant
            for j in range(3)
        ]
    )


def face_flux(field, faces, trans, back):
    x_next, x_prev, y_next, y_prev, z_next, z_prev = faces
    padded = jnp.concatenate([x_prev, field, x_next], 0)
    rim_x = ((1, 1), (0, 0), (0, 0))
    padded = jnp.concatenate([jnp.pad(y_prev, rim_x), padded, jnp.pad(y_next, rim_x)], 1)
    rim_xy = ((1, 1), (1, 1), (0, 0))
    padded = jnp.concatenate([jnp.pad(z_prev, rim_xy), padded, jnp.pad(z_next, rim_xy)], 2)
    total = trans[0] * (field - padded[2:, 1:-1, 1:-1]) + back[0] * (
        field - padded[:-2, 1:-1, 1:-1]
    )
    total = (
        total
        + trans[1] * (field - padded[1:-1, 2:, 1:-1])
        + back[1] * (field - padded[1:-1, :-2, 1:-1])
    )
    total = (
        total
        + trans[2] * (field - padded[1:-1, 1:-1, 2:])
        + back[2] * (field - padded[1:-1, 1:-1, :-2])
    )
    return total


def coarse_step(coarse, rhs_total, coefs, padded):
    dsum, plus_x, minus_x, plus_y, minus_y, plus_z, minus_z, cdiag = coefs
    applied = (
        dsum * coarse
        + plus_x * (coarse - padded[2:, 1:-1, 1:-1])
        + minus_x * (coarse - padded[:-2, 1:-1, 1:-1])
    )
    applied = (
        applied
        + plus_y * (coarse - padded[1:-1, 2:, 1:-1])
        + minus_y * (coarse - padded[1:-1, :-2, 1:-1])
    )
    applied = (
        applied
        + plus_z * (coarse - padded[1:-1, 1:-1, 2:])
        + minus_z * (coarse - padded[1:-1, 1:-1, :-2])
    )
    return coarse + omega_coarse * (rhs_total - applied) / cdiag


def least_squares(beta, h11, h21, h12, h22, h32):
    r11 = jnp.sqrt(h11 * h11 + h21 * h21)
    cos_one = h11 / r11
    sin_one = h21 / r11
    g_first = cos_one * beta
    g_second = -sin_one * beta
    upper = cos_one * h12 + sin_one * h22
    lower = cos_one * h22 - sin_one * h12
    r22 = jnp.sqrt(lower * lower + h32 * h32)
    second = lower * g_second / (r22 * r22)
    first = (g_first - upper * second) / r11
    return (first, second)


def shards(residual_eq, diag_block, mobility, trans, perf_cell, perf_well, perf_index):
    size_x = lax.axis_size("gx")
    size_y = lax.axis_size("gy")
    size_z = lax.axis_size("gz")
    cx, cy, cz = trans.shape[1:]
    ix = lax.axis_index("gx")
    iy = lax.axis_index("gy")
    iz = lax.axis_index("gz")

    local_well = perf_well[:, 0] - (device_number() - 1) * WELL_DEV

    slot_of_well = local_well[:, None] == jnp.arange(2 * WELL_DEV, dtype=local_well.dtype)[None, :]

    def well_partials(values):
        return jnp.sum(jnp.where(slot_of_well, values[:, None], 0.0), axis=0)

    def per_slot(table):
        return jnp.sum(jnp.where(slot_of_well, table[None, :], 0.0), axis=1)

    def exchange(field, partial):
        x_next = send_down(field[:1], "gx")
        x_prev = send_up(field[-1:], "gx")
        y_next = send_down(field[:, :1], "gy")
        y_prev = send_up(field[:, -1:], "gy")
        down = jnp.concatenate([field[:, :, 0].reshape(-1), partial[:WELL_DEV]])
        up = jnp.concatenate([field[:, :, -1].reshape(-1), partial[WELL_DEV:]])
        from_next = send_down(down, "gz")
        from_prev = send_up(up, "gz")
        z_next = from_next[: cx * cy].reshape(cx, cy, 1)
        z_prev = from_prev[: cx * cy].reshape(cx, cy, 1)
        totals = partial + jnp.concatenate([from_prev[cx * cy :], from_next[cx * cy :]])
        return (x_next, x_prev, y_next, y_prev, z_next, z_prev), totals

    weight_part = well_partials(perf_index)
    faces_t, weights = exchange(trans[2], weight_part)
    layer_x = send_up(trans[0, -1:], "gx")
    layer_y = send_up(trans[1][:, -1:], "gy")
    layer_z = faces_t[5]
    back = jnp.stack(
        [
            jnp.concatenate([layer_x, trans[0, :-1]], 0),
            jnp.concatenate([layer_y, trans[1][:, :-1]], 1),
            jnp.concatenate([layer_z, trans[2][:, :, :-1]], 2),
        ]
    )

    def flux(field, faces):
        return face_flux(field, faces, trans, back)

    def flux_wells(field):
        flat = field.reshape(-1)
        values = flat[perf_cell]
        faces, totals = exchange(field, well_partials(perf_index * values))
        bottom = per_slot(totals / weights)
        terms = perf_index * (values - bottom)
        wells = jnp.zeros_like(flat).at[perf_cell].add(terms).reshape(field.shape)
        return flux(field, faces) + wells

    def jacobian(vector):
        coupling = flux_wells(vector[0])
        return (
            diag_block[:, 0] * vector[0]
            + diag_block[:, 1] * vector[1]
            + diag_block[:, 2] * vector[2]
            + mobility * coupling[None]
        )

    dpress = diag_block[0, 0] + diag_block[1, 0] + diag_block[2, 0]
    lam = mobility[0] + mobility[1] + mobility[2]
    pdiag = dpress + lam * (trans[0] + back[0] + trans[1] + back[1] + trans[2] + back[2])
    dsum = jnp.sum(dpress)
    plus_x = jnp.sum(lam[-1] * trans[0, -1])
    minus_x = jnp.sum(lam[0] * back[0, 0])
    plus_y = jnp.sum(lam[:, -1] * trans[1][:, -1])
    minus_y = jnp.sum(lam[:, 0] * back[1][:, 0])
    plus_z = jnp.sum(lam[:, :, -1] * trans[2][:, :, -1])
    minus_z = jnp.sum(lam[:, :, 0] * back[2][:, :, 0])

    rhs = -residual_eq
    start = gather_all(
        jnp.stack(
            [
                jnp.sum(rhs * rhs),
                jnp.sum(rhs[0] + rhs[1] + rhs[2]),
                dsum,
                plus_x,
                minus_x,
                plus_y,
                minus_y,
                plus_z,
                minus_z,
            ]
        )
    )
    grid = (size_x, size_y, size_z)
    beta = jnp.sqrt(jnp.sum(start[:, 0]))
    coarse_coefs = [start[:, k].reshape(grid) for k in range(2, 9)]
    cdiag = coarse_coefs[0]
    for value in coarse_coefs[1:]:
        cdiag = cdiag + value
    coarse_coefs = tuple(coarse_coefs) + (cdiag,)

    def coarse_solve(rhs_total):
        coarse = jnp.zeros(grid, jnp.float32)
        for sweep in range(CSWEEPS):
            coarse = coarse_step(coarse, rhs_total, coarse_coefs, jnp.pad(coarse, 1))
        padded = jnp.pad(coarse, 1)

        def at(dx, dy, dz):
            return padded[ix + 1 + dx, iy + 1 + dy, iz + 1 + dz]

        faces = (
            jnp.broadcast_to(at(1, 0, 0), (1, cy, cz)),
            jnp.broadcast_to(at(-1, 0, 0), (1, cy, cz)),
            jnp.broadcast_to(at(0, 1, 0), (cx, 1, cz)),
            jnp.broadcast_to(at(0, -1, 0), (cx, 1, cz)),
            jnp.broadcast_to(at(0, 0, 1), (cx, cy, 1)),
            jnp.broadcast_to(at(0, 0, -1), (cx, cy, 1)),
        )
        return at(0, 0, 0), faces

    def precondition(vector, rhs_total):
        rpress = vector[0] + vector[1] + vector[2]
        own, faces = coarse_solve(rhs_total)
        press = jnp.broadcast_to(own, rpress.shape)
        for sweep in range(FSWEEPS):
            if sweep:
                faces, _ = exchange(press, jnp.zeros((2 * WELL_DEV,), jnp.float32))
            press = press + omega_fine * (rpress - (dpress * press + lam * flux(press, faces))) / pdiag
        coupling = flux_wells(press)
        applied = diag_block[:, 0] * press + mobility * coupling[None]
        correction = block_solve(diag_block, vector - applied)
        return jnp.concatenate([(correction[0] + press)[None], correction[1:]], 0)

    first_basis = rhs / beta
    first_dir = precondition(first_basis, start[:, 1].reshape(grid) / beta)
    work = jacobian(first_dir)
    second = gather_all(
        jnp.stack(
            [
                jnp.sum(first_basis * work),
                jnp.sum(work * work),
                jnp.sum(first_basis * first_basis),
                jnp.sum(work[0] + work[1] + work[2]),
            ]
        )
    )
    h11 = jnp.sum(second[:, 0])
    norm_v1 = jnp.sum(second[:, 2])
    h21 = jnp.sqrt(jnp.sum(second[:, 1]) - 2.0 * h11 * h11 + h11 * h11 * norm_v1)
    applied_dir = precondition(work, second[:, 3].reshape(grid))
    second_basis = (work - h11 * first_basis) / h21
    second_dir = (applied_dir - h11 * first_dir) / h21
    work = jacobian(second_dir)
    sums = allsum(
        jnp.stack(
            [
                jnp.sum(first_basis * work),
                jnp.sum(second_basis * work),
                jnp.sum(work * work),
                jnp.sum(second_basis * second_basis),
                jnp.sum(first_basis * second_basis),
            ]
        )
    )
    h12 = sums[0]
    h22 = sums[1]
    h32 = jnp.sqrt(
        sums[2]
        + h12 * h12 * norm_v1
        + h22 * h22 * sums[3]
        - 2.0 * h12 * h12
        - 2.0 * h22 * h22
        + 2.0 * h12 * h22 * sums[4]
    )
    first, second = least_squares(beta, h11, h21, h12, h22, h32)
    return first * first_dir + second * second_dir


def solution(mesh):
    in_specs = (
        P(None, "gx", "gy", "gz"),
        P(None, None, "gx", "gy", "gz"),
        P(None, "gx", "gy", "gz"),
        P(None, "gx", "gy", "gz"),
        P(("gx", "gy", "gz")),
        P(("gx", "gy", "gz"), None),
        P(("gx", "gy", "gz")),
    )
    out_specs = P(None, "gx", "gy", "gz")
    return jax.shard_map(shards, mesh=mesh, in_specs=in_specs, out_specs=out_specs, check_vma=False)
```

```python
import jax
import jax.numpy as jnp
from jax import lax
from jax.sharding import PartitionSpec as P

WELL_DEV = 20
CSWEEPS = 4
FSWEEPS = 6


omega_fine = 0.7
omega_coarse = 0.7

AXES = ("gx", "gy", "gz")


def send_up(block, axis):
    size = lax.axis_size(axis)
    moved = lax.ppermute(block, axis, [(i, (i + 1) % size) for i in range(size)])
    return jnp.where(lax.axis_index(axis) == 0, jnp.zeros_like(moved), moved)


def send_down(block, axis):
    size = lax.axis_size(axis)
    moved = lax.ppermute(block, axis, [(i, (i - 1) % size) for i in range(size)])
    return jnp.where(lax.axis_index(axis) == size - 1, jnp.zeros_like(moved), moved)


def allsum(value):
    for axis in reversed(AXES):
        size = lax.axis_size(axis)
        if size & (size - 1):
            value = lax.psum(value, axis)
            continue
        step = 1
        while step < size:
            value = value + lax.ppermute(value, axis, [(i, i ^ step) for i in range(size)])
            step *= 2
    return value


def device_number():
    return (lax.axis_index("gx") * lax.axis_size("gy") + lax.axis_index("gy")) * lax.axis_size(
        "gz"
    ) + lax.axis_index("gz")


def gather_all(local):
    count = lax.axis_size("gx") * lax.axis_size("gy") * lax.axis_size("gz")
    slots = jnp.zeros((count, local.shape[0]), local.dtype).at[device_number()].set(local)
    return allsum(slots)


def block_solve(blocks, rhs):
    matrix = [[blocks[i, j] for j in range(3)] for i in range(3)]

    def cofactor(i, j):
        return (
            matrix[(i + 1) % 3][(j + 1) % 3] * matrix[(i + 2) % 3][(j + 2) % 3]
            - matrix[(i + 1) % 3][(j + 2) % 3] * matrix[(i + 2) % 3][(j + 1) % 3]
        )

    cofs = [[cofactor(i, j) for j in range(3)] for i in range(3)]
    determinant = matrix[0][0] * cofs[0][0] + matrix[0][1] * cofs[0][1] + matrix[0][2] * cofs[0][2]
    return jnp.stack(
        [
            (cofs[0][j] * rhs[0] + cofs[1][j] * rhs[1] + cofs[2][j] * rhs[2]) / determinant
            for j in range(3)
        ]
    )


def face_flux(field, faces, trans, back):
    x_next, x_prev, y_next, y_prev, z_next, z_prev = faces
    padded = jnp.concatenate([x_prev, field, x_next], 0)
    rim_x = ((1, 1), (0, 0), (0, 0))
    padded = jnp.concatenate([jnp.pad(y_prev, rim_x), padded, jnp.pad(y_next, rim_x)], 1)
    rim_xy = ((1, 1), (1, 1), (0, 0))
    padded = jnp.concatenate([jnp.pad(z_prev, rim_xy), padded, jnp.pad(z_next, rim_xy)], 2)
    total = trans[0] * (field - padded[2:, 1:-1, 1:-1]) + back[0] * (
        field - padded[:-2, 1:-1, 1:-1]
    )
    total = (
        total
        + trans[1] * (field - padded[1:-1, 2:, 1:-1])
        + back[1] * (field - padded[1:-1, :-2, 1:-1])
    )
    total = (
        total
        + trans[2] * (field - padded[1:-1, 1:-1, 2:])
        + back[2] * (field - padded[1:-1, 1:-1, :-2])
    )
    return total


def coarse_step(coarse, rhs_total, coefs, padded):
    dsum, plus_x, minus_x, plus_y, minus_y, plus_z, minus_z, cdiag = coefs
    applied = (
        dsum * coarse
        + plus_x * (coarse - padded[2:, 1:-1, 1:-1])
        + minus_x * (coarse - padded[:-2, 1:-1, 1:-1])
    )
    applied = (
        applied
        + plus_y * (coarse - padded[1:-1, 2:, 1:-1])
        + minus_y * (coarse - padded[1:-1, :-2, 1:-1])
    )
    applied = (
        applied
        + plus_z * (coarse - padded[1:-1, 1:-1, 2:])
        + minus_z * (coarse - padded[1:-1, 1:-1, :-2])
    )
    return coarse + omega_coarse * (rhs_total - applied) / cdiag


def least_squares(beta, h11, h21, h12, h22, h32):
    r11 = jnp.sqrt(h11 * h11 + h21 * h21)
    cos_one = h11 / r11
    sin_one = h21 / r11
    g_first = cos_one * beta
    g_second = -sin_one * beta
    upper = cos_one * h12 + sin_one * h22
    lower = cos_one * h22 - sin_one * h12
    r22 = jnp.sqrt(lower * lower + h32 * h32)
    second = lower * g_second / (r22 * r22)
    first = (g_first - upper * second) / r11
    return (first, second)


def shards(residual_eq, diag_block, mobility, trans, perf_cell, perf_well, perf_index):
    size_x = lax.axis_size("gx")
    size_y = lax.axis_size("gy")
    size_z = lax.axis_size("gz")
    cx, cy, cz = trans.shape[1:]
    ix = lax.axis_index("gx")
    iy = lax.axis_index("gy")
    iz = lax.axis_index("gz")

    local_well = perf_well[:, 0] - (device_number() - 1) * WELL_DEV

    slot_of_well = local_well[:, None] == jnp.arange(2 * WELL_DEV, dtype=local_well.dtype)[None, :]

    def well_partials(values):
        return jnp.sum(jnp.where(slot_of_well, values[:, None], 0.0), axis=0)

    def per_slot(table):
        return jnp.sum(jnp.where(slot_of_well, table[None, :], 0.0), axis=1)

    def exchange(field, partial):
        x_next = send_down(field[:1], "gx")
        x_prev = send_up(field[-1:], "gx")
        y_next = send_down(field[:, :1], "gy")
        y_prev = send_up(field[:, -1:], "gy")
        down = jnp.concatenate([field[:, :, 0].reshape(-1), partial[:WELL_DEV]])
        up = jnp.concatenate([field[:, :, -1].reshape(-1), partial[WELL_DEV:]])
        from_next = send_down(down, "gz")
        from_prev = send_up(up, "gz")
        z_next = from_next[: cx * cy].reshape(cx, cy, 1)
        z_prev = from_prev[: cx * cy].reshape(cx, cy, 1)
        totals = partial + jnp.concatenate([from_prev[cx * cy :], from_next[cx * cy :]])
        return (x_next, x_prev, y_next, y_prev, z_next, z_prev), totals

    weight_part = well_partials(perf_index)
    faces_t, weights = exchange(trans[2], weight_part)
    layer_x = send_up(trans[0, -1:], "gx")
    layer_y = send_up(trans[1][:, -1:], "gy")
    layer_z = faces_t[5]
    back = jnp.stack(
        [
            jnp.concatenate([layer_x, trans[0, :-1]], 0),
            jnp.concatenate([layer_y, trans[1][:, :-1]], 1),
            jnp.concatenate([layer_z, trans[2][:, :, :-1]], 2),
        ]
    )

    def flux(field, faces):
        return face_flux(field, faces, trans, back)

    def flux_wells(field):
        flat = field.reshape(-1)
        values = flat[perf_cell]
        faces, totals = exchange(field, well_partials(perf_index * values))
        bottom = per_slot(totals / weights)
        terms = perf_index * (values - bottom)
        wells = jnp.zeros_like(flat).at[perf_cell].add(terms).reshape(field.shape)
        return flux(field, faces) + wells

    def jacobian(vector):
        coupling = flux_wells(vector[0])
        return (
            diag_block[:, 0] * vector[0]
            + diag_block[:, 1] * vector[1]
            + diag_block[:, 2] * vector[2]
            + mobility * coupling[None]
        )

    dpress = diag_block[0, 0] + diag_block[1, 0] + diag_block[2, 0]
    lam = mobility[0] + mobility[1] + mobility[2]
    pdiag = dpress + lam * (trans[0] + back[0] + trans[1] + back[1] + trans[2] + back[2])
    dsum = jnp.sum(dpress)
    plus_x = jnp.sum(lam[-1] * trans[0, -1])
    minus_x = jnp.sum(lam[0] * back[0, 0])
    plus_y = jnp.sum(lam[:, -1] * trans[1][:, -1])
    minus_y = jnp.sum(lam[:, 0] * back[1][:, 0])
    plus_z = jnp.sum(lam[:, :, -1] * trans[2][:, :, -1])
    minus_z = jnp.sum(lam[:, :, 0] * back[2][:, :, 0])

    rhs = -residual_eq
    start = gather_all(
        jnp.stack(
            [
                jnp.sum(rhs * rhs),
                jnp.sum(rhs[0] + rhs[1] + rhs[2]),
                dsum,
                plus_x,
                minus_x,
                plus_y,
                minus_y,
                plus_z,
                minus_z,
            ]
        )
    )
    grid = (size_x, size_y, size_z)
    beta = jnp.sqrt(jnp.sum(start[:, 0]))
    coarse_coefs = [start[:, k].reshape(grid) for k in range(2, 9)]
    cdiag = coarse_coefs[0]
    for value in coarse_coefs[1:]:
        cdiag = cdiag + value
    coarse_coefs = tuple(coarse_coefs) + (cdiag,)

    def coarse_solve(rhs_total):
        coarse = jnp.zeros(grid, jnp.float32)
        for sweep in range(CSWEEPS):
            coarse = coarse_step(coarse, rhs_total, coarse_coefs, jnp.pad(coarse, 1))
        padded = jnp.pad(coarse, 1)

        def at(dx, dy, dz):
            return padded[ix + 1 + dx, iy + 1 + dy, iz + 1 + dz]

        faces = (
            jnp.broadcast_to(at(1, 0, 0), (1, cy, cz)),
            jnp.broadcast_to(at(-1, 0, 0), (1, cy, cz)),
            jnp.broadcast_to(at(0, 1, 0), (cx, 1, cz)),
            jnp.broadcast_to(at(0, -1, 0), (cx, 1, cz)),
            jnp.broadcast_to(at(0, 0, 1), (cx, cy, 1)),
            jnp.broadcast_to(at(0, 0, -1), (cx, cy, 1)),
        )
        return at(0, 0, 0), faces

    def precondition(vector, rhs_total):
        rpress = vector[0] + vector[1] + vector[2]
        own, faces = coarse_solve(rhs_total)
        press = jnp.broadcast_to(own, rpress.shape)
        for sweep in range(FSWEEPS):
            if sweep:
                faces, _ = exchange(press, jnp.zeros((2 * WELL_DEV,), jnp.float32))
            press = press + omega_fine * (rpress - (dpress * press + lam * flux(press, faces))) / pdiag
        coupling = flux_wells(press)
        applied = diag_block[:, 0] * press + mobility * coupling[None]
        correction = block_solve(diag_block, vector - applied)
        return jnp.concatenate([(correction[0] + press)[None], correction[1:]], 0)

    first_basis = rhs / beta
    first_dir = precondition(first_basis, start[:, 1].reshape(grid) / beta)
    work = jacobian(first_dir)
    second = gather_all(
        jnp.stack(
            [
                jnp.sum(first_basis * work),
                jnp.sum(work * work),
                jnp.sum(first_basis * first_basis),
                jnp.sum(work[0] + work[1] + work[2]),
            ]
        )
    )
    h11 = jnp.sum(second[:, 0])
    norm_v1 = jnp.sum(second[:, 2])
    h21 = jnp.sqrt(jnp.sum(second[:, 1]) - 2.0 * h11 * h11 + h11 * h11 * norm_v1)
    applied_dir = precondition(work, second[:, 3].reshape(grid))
    second_basis = (work - h11 * first_basis) / h21
    second_dir = (applied_dir - h11 * first_dir) / h21
    work = jacobian(second_dir)
    sums = allsum(
        jnp.stack(
            [
                jnp.sum(first_basis * work),
                jnp.sum(second_basis * work),
                jnp.sum(work * work),
                jnp.sum(second_basis * second_basis),
                jnp.sum(first_basis * second_basis),
            ]
        )
    )
    h12 = sums[0]
    h22 = sums[1]
    h32 = jnp.sqrt(
        sums[2]
        + h12 * h12 * norm_v1
        + h22 * h22 * sums[3]
        - 2.0 * h12 * h12
        - 2.0 * h22 * h22
        + 2.0 * h12 * h22 * sums[4]
    )
    first, second = least_squares(beta, h11, h21, h12, h22, h32)
    return first * first_dir + second * second_dir


def solution(mesh):
    in_specs = (
        P(None, "gx", "gy", "gz"),
        P(None, None, "gx", "gy", "gz"),
        P(None, "gx", "gy", "gz"),
        P(None, "gx", "gy", "gz"),
        P(("gx", "gy", "gz")),
        P(("gx", "gy", "gz"), None),
        P(("gx", "gy", "gz")),
    )
    out_specs = P(None, "gx", "gy", "gz")
    return jax.shard_map(shards, mesh=mesh, in_specs=in_specs, out_specs=out_specs, check_vma=False)
```

```python
import jax
import jax.numpy as jnp
from jax import lax
from jax.sharding import PartitionSpec as P

WELL_DEV = 20
CSWEEPS = 4
FSWEEPS = 6


omega_fine = 0.7
omega_coarse = 0.7

AXES = ("gx", "gy", "gz")


def send_up(block, axis):
    size = lax.axis_size(axis)
    moved = lax.ppermute(block, axis, [(i, (i + 1) % size) for i in range(size)])
    return jnp.where(lax.axis_index(axis) == 0, jnp.zeros_like(moved), moved)


def send_down(block, axis):
    size = lax.axis_size(axis)
    moved = lax.ppermute(block, axis, [(i, (i - 1) % size) for i in range(size)])
    return jnp.where(lax.axis_index(axis) == size - 1, jnp.zeros_like(moved), moved)


def allsum(value):
    for axis in reversed(AXES):
        size = lax.axis_size(axis)
        if size & (size - 1):
            value = lax.psum(value, axis)
            continue
        step = 1
        while step < size:
            value = value + lax.ppermute(value, axis, [(i, i ^ step) for i in range(size)])
            step *= 2
    return value


def device_number():
    return (lax.axis_index("gx") * lax.axis_size("gy") + lax.axis_index("gy")) * lax.axis_size(
        "gz"
    ) + lax.axis_index("gz")


def gather_all(local):
    count = lax.axis_size("gx") * lax.axis_size("gy") * lax.axis_size("gz")
    slots = jnp.zeros((count, local.shape[0]), local.dtype).at[device_number()].set(local)
    return allsum(slots)


def block_solve(blocks, rhs):
    matrix = [[blocks[i, j] for j in range(3)] for i in range(3)]

    def cofactor(i, j):
        return (
            matrix[(i + 1) % 3][(j + 1) % 3] * matrix[(i + 2) % 3][(j + 2) % 3]
            - matrix[(i + 1) % 3][(j + 2) % 3] * matrix[(i + 2) % 3][(j + 1) % 3]
        )

    cofs = [[cofactor(i, j) for j in range(3)] for i in range(3)]
    determinant = matrix[0][0] * cofs[0][0] + matrix[0][1] * cofs[0][1] + matrix[0][2] * cofs[0][2]
    return jnp.stack(
        [
            (cofs[0][j] * rhs[0] + cofs[1][j] * rhs[1] + cofs[2][j] * rhs[2]) / determinant
            for j in range(3)
        ]
    )


def face_flux(field, faces, trans, back):
    x_next, x_prev, y_next, y_prev, z_next, z_prev = faces
    padded = jnp.concatenate([x_prev, field, x_next], 0)
    rim_x = ((1, 1), (0, 0), (0, 0))
    padded = jnp.concatenate([jnp.pad(y_prev, rim_x), padded, jnp.pad(y_next, rim_x)], 1)
    rim_xy = ((1, 1), (1, 1), (0, 0))
    padded = jnp.concatenate([jnp.pad(z_prev, rim_xy), padded, jnp.pad(z_next, rim_xy)], 2)
    total = trans[0] * (field - padded[2:, 1:-1, 1:-1]) + back[0] * (
        field - padded[:-2, 1:-1, 1:-1]
    )
    total = (
        total
        + trans[1] * (field - padded[1:-1, 2:, 1:-1])
        + back[1] * (field - padded[1:-1, :-2, 1:-1])
    )
    total = (
        total
        + trans[2] * (field - padded[1:-1, 1:-1, 2:])
        + back[2] * (field - padded[1:-1, 1:-1, :-2])
    )
    return total


def coarse_step(coarse, rhs_total, coefs, padded):
    dsum, plus_x, minus_x, plus_y, minus_y, plus_z, minus_z, cdiag = coefs
    applied = (
        dsum * coarse
        + plus_x * (coarse - padded[2:, 1:-1, 1:-1])
        + minus_x * (coarse - padded[:-2, 1:-1, 1:-1])
    )
    applied = (
        applied
        + plus_y * (coarse - padded[1:-1, 2:, 1:-1])
        + minus_y * (coarse - padded[1:-1, :-2, 1:-1])
    )
    applied = (
        applied
        + plus_z * (coarse - padded[1:-1, 1:-1, 2:])
        + minus_z * (coarse - padded[1:-1, 1:-1, :-2])
    )
    return coarse + omega_coarse * (rhs_total - applied) / cdiag


def least_squares(beta, h11, h21, h12, h22, h32):
    r11 = jnp.sqrt(h11 * h11 + h21 * h21)
    cos_one = h11 / r11
    sin_one = h21 / r11
    g_first = cos_one * beta
    g_second = -sin_one * beta
    upper = cos_one * h12 + sin_one * h22
    lower = cos_one * h22 - sin_one * h12
    r22 = jnp.sqrt(lower * lower + h32 * h32)
    second = lower * g_second / (r22 * r22)
    first = (g_first - upper * second) / r11
    return (first, second)


def shards(residual_eq, diag_block, mobility, trans, perf_cell, perf_well, perf_index):
    size_x = lax.axis_size("gx")
    size_y = lax.axis_size("gy")
    size_z = lax.axis_size("gz")
    cx, cy, cz = trans.shape[1:]
    ix = lax.axis_index("gx")
    iy = lax.axis_index("gy")
    iz = lax.axis_index("gz")

    local_well = perf_well[:, 0] - (device_number() - 1) * WELL_DEV

    slot_of_well = local_well[:, None] == jnp.arange(2 * WELL_DEV, dtype=local_well.dtype)[None, :]

    def well_partials(values):
        return jnp.sum(jnp.where(slot_of_well, values[:, None], 0.0), axis=0)

    def per_slot(table):
        return jnp.sum(jnp.where(slot_of_well, table[None, :], 0.0), axis=1)

    def exchange(field, partial):
        x_next = send_down(field[:1], "gx")
        x_prev = send_up(field[-1:], "gx")
        y_next = send_down(field[:, :1], "gy")
        y_prev = send_up(field[:, -1:], "gy")
        if partial is None:
            z_next = send_down(field[:, :, :1], "gz")
            z_prev = send_up(field[:, :, -1:], "gz")
            return (x_next, x_prev, y_next, y_prev, z_next, z_prev), None
        down = jnp.concatenate([field[:, :, 0].reshape(-1), partial[:WELL_DEV]])
        up = jnp.concatenate([field[:, :, -1].reshape(-1), partial[WELL_DEV:]])
        from_next = send_down(down, "gz")
        from_prev = send_up(up, "gz")
        z_next = from_next[: cx * cy].reshape(cx, cy, 1)
        z_prev = from_prev[: cx * cy].reshape(cx, cy, 1)
        totals = partial + jnp.concatenate([from_prev[cx * cy :], from_next[cx * cy :]])
        return (x_next, x_prev, y_next, y_prev, z_next, z_prev), totals

    weight_part = well_partials(perf_index)
    faces_t, weights = exchange(trans[2], weight_part)
    layer_x = send_up(trans[0, -1:], "gx")
    layer_y = send_up(trans[1][:, -1:], "gy")
    layer_z = faces_t[5]
    back = jnp.stack(
        [
            jnp.concatenate([layer_x, trans[0, :-1]], 0),
            jnp.concatenate([layer_y, trans[1][:, :-1]], 1),
            jnp.concatenate([layer_z, trans[2][:, :, :-1]], 2),
        ]
    )

    def flux(field, faces):
        return face_flux(field, faces, trans, back)

    def flux_wells(field):
        flat = field.reshape(-1)
        values = flat[perf_cell]
        faces, totals = exchange(field, well_partials(perf_index * values))
        bottom = per_slot(totals / weights)
        terms = perf_index * (values - bottom)
        wells = jnp.zeros_like(flat).at[perf_cell].add(terms).reshape(field.shape)
        return flux(field, faces) + wells

    def jacobian(vector):
        coupling = flux_wells(vector[0])
        return (
            diag_block[:, 0] * vector[0]
            + diag_block[:, 1] * vector[1]
            + diag_block[:, 2] * vector[2]
            + mobility * coupling[None]
        )

    dpress = diag_block[0, 0] + diag_block[1, 0] + diag_block[2, 0]
    lam = mobility[0] + mobility[1] + mobility[2]
    pdiag = dpress + lam * (trans[0] + back[0] + trans[1] + back[1] + trans[2] + back[2])
    dsum = jnp.sum(dpress)
    plus_x = jnp.sum(lam[-1] * trans[0, -1])
    minus_x = jnp.sum(lam[0] * back[0, 0])
    plus_y = jnp.sum(lam[:, -1] * trans[1][:, -1])
    minus_y = jnp.sum(lam[:, 0] * back[1][:, 0])
    plus_z = jnp.sum(lam[:, :, -1] * trans[2][:, :, -1])
    minus_z = jnp.sum(lam[:, :, 0] * back[2][:, :, 0])

    rhs = -residual_eq
    start = gather_all(
        jnp.stack(
            [
                jnp.sum(rhs * rhs),
                jnp.sum(rhs[0] + rhs[1] + rhs[2]),
                dsum,
                plus_x,
                minus_x,
                plus_y,
                minus_y,
                plus_z,
                minus_z,
            ]
        )
    )
    grid = (size_x, size_y, size_z)
    beta = jnp.sqrt(jnp.sum(start[:, 0]))
    coarse_coefs = [start[:, k].reshape(grid) for k in range(2, 9)]
    cdiag = coarse_coefs[0]
    for value in coarse_coefs[1:]:
        cdiag = cdiag + value
    coarse_coefs = tuple(coarse_coefs) + (cdiag,)

    def coarse_solve(rhs_total):
        coarse = jnp.zeros(grid, jnp.float32)
        for sweep in range(CSWEEPS):
            coarse = coarse_step(coarse, rhs_total, coarse_coefs, jnp.pad(coarse, 1))
        padded = jnp.pad(coarse, 1)

        def at(dx, dy, dz):
            return padded[ix + 1 + dx, iy + 1 + dy, iz + 1 + dz]

        faces = (
            jnp.broadcast_to(at(1, 0, 0), (1, cy, cz)),
            jnp.broadcast_to(at(-1, 0, 0), (1, cy, cz)),
            jnp.broadcast_to(at(0, 1, 0), (cx, 1, cz)),
            jnp.broadcast_to(at(0, -1, 0), (cx, 1, cz)),
            jnp.broadcast_to(at(0, 0, 1), (cx, cy, 1)),
            jnp.broadcast_to(at(0, 0, -1), (cx, cy, 1)),
        )
        return at(0, 0, 0), faces

    def precondition(vector, rhs_total):
        rpress = vector[0] + vector[1] + vector[2]
        own, faces = coarse_solve(rhs_total)
        press = jnp.broadcast_to(own, rpress.shape)
        for sweep in range(FSWEEPS):
            if sweep:
                faces, _ = exchange(press, None)
            press = press + omega_fine * (rpress - (dpress * press + lam * flux(press, faces))) / pdiag
        coupling = flux_wells(press)
        applied = diag_block[:, 0] * press + mobility * coupling[None]
        correction = block_solve(diag_block, vector - applied)
        return jnp.concatenate([(correction[0] + press)[None], correction[1:]], 0)

    first_basis = rhs / beta
    first_dir = precondition(first_basis, start[:, 1].reshape(grid) / beta)
    work = jacobian(first_dir)
    second = gather_all(
        jnp.stack(
            [
                jnp.sum(first_basis * work),
                jnp.sum(work * work),
                jnp.sum(first_basis * first_basis),
                jnp.sum(work[0] + work[1] + work[2]),
            ]
        )
    )
    h11 = jnp.sum(second[:, 0])
    norm_v1 = jnp.sum(second[:, 2])
    h21 = jnp.sqrt(jnp.sum(second[:, 1]) - 2.0 * h11 * h11 + h11 * h11 * norm_v1)
    applied_dir = precondition(work, second[:, 3].reshape(grid))
    second_basis = (work - h11 * first_basis) / h21
    second_dir = (applied_dir - h11 * first_dir) / h21
    work = jacobian(second_dir)
    sums = allsum(
        jnp.stack(
            [
                jnp.sum(first_basis * work),
                jnp.sum(second_basis * work),
                jnp.sum(work * work),
                jnp.sum(second_basis * second_basis),
                jnp.sum(first_basis * second_basis),
            ]
        )
    )
    h12 = sums[0]
    h22 = sums[1]
    h32 = jnp.sqrt(
        sums[2]
        + h12 * h12 * norm_v1
        + h22 * h22 * sums[3]
        - 2.0 * h12 * h12
        - 2.0 * h22 * h22
        + 2.0 * h12 * h22 * sums[4]
    )
    first, second = least_squares(beta, h11, h21, h12, h22, h32)
    return first * first_dir + second * second_dir


def solution(mesh):
    in_specs = (
        P(None, "gx", "gy", "gz"),
        P(None, None, "gx", "gy", "gz"),
        P(None, "gx", "gy", "gz"),
        P(None, "gx", "gy", "gz"),
        P(("gx", "gy", "gz")),
        P(("gx", "gy", "gz"), None),
        P(("gx", "gy", "gz")),
    )
    out_specs = P(None, "gx", "gy", "gz")
    return jax.shard_map(shards, mesh=mesh, in_specs=in_specs, out_specs=out_specs, check_vma=False)
```

```python
import jax
import jax.numpy as jnp
from jax import lax
from jax.sharding import PartitionSpec as P

WELL_DEV = 20
CSWEEPS = 4
FSWEEPS = 6


omega_fine = 0.7
omega_coarse = 0.7

AXES = ("gx", "gy", "gz")


def send_up(block, axis):
    size = lax.axis_size(axis)
    moved = lax.ppermute(block, axis, [(i, (i + 1) % size) for i in range(size)])
    return jnp.where(lax.axis_index(axis) == 0, jnp.zeros_like(moved), moved)


def send_down(block, axis):
    size = lax.axis_size(axis)
    moved = lax.ppermute(block, axis, [(i, (i - 1) % size) for i in range(size)])
    return jnp.where(lax.axis_index(axis) == size - 1, jnp.zeros_like(moved), moved)


def allsum(value):
    for axis in reversed(AXES):
        size = lax.axis_size(axis)
        if size & (size - 1):
            value = lax.psum(value, axis)
            continue
        step = 1
        while step < size:
            value = value + lax.ppermute(value, axis, [(i, i ^ step) for i in range(size)])
            step *= 2
    return value


def device_number():
    return (lax.axis_index("gx") * lax.axis_size("gy") + lax.axis_index("gy")) * lax.axis_size(
        "gz"
    ) + lax.axis_index("gz")


def gather_all(local):
    count = lax.axis_size("gx") * lax.axis_size("gy") * lax.axis_size("gz")
    slots = jnp.zeros((count, local.shape[0]), local.dtype).at[device_number()].set(local)
    return allsum(slots)


def block_solve(blocks, rhs):
    matrix = [[blocks[i, j] for j in range(3)] for i in range(3)]

    def cofactor(i, j):
        return (
            matrix[(i + 1) % 3][(j + 1) % 3] * matrix[(i + 2) % 3][(j + 2) % 3]
            - matrix[(i + 1) % 3][(j + 2) % 3] * matrix[(i + 2) % 3][(j + 1) % 3]
        )

    cofs = [[cofactor(i, j) for j in range(3)] for i in range(3)]
    determinant = matrix[0][0] * cofs[0][0] + matrix[0][1] * cofs[0][1] + matrix[0][2] * cofs[0][2]
    return jnp.stack(
        [
            (cofs[0][j] * rhs[0] + cofs[1][j] * rhs[1] + cofs[2][j] * rhs[2]) / determinant
            for j in range(3)
        ]
    )


def face_flux(field, faces, trans, back):
    x_next, x_prev, y_next, y_prev, z_next, z_prev = faces
    padded = jnp.concatenate([x_prev, field, x_next], 0)
    rim_x = ((1, 1), (0, 0), (0, 0))
    padded = jnp.concatenate([jnp.pad(y_prev, rim_x), padded, jnp.pad(y_next, rim_x)], 1)
    rim_xy = ((1, 1), (1, 1), (0, 0))
    padded = jnp.concatenate([jnp.pad(z_prev, rim_xy), padded, jnp.pad(z_next, rim_xy)], 2)
    total = trans[0] * (field - padded[2:, 1:-1, 1:-1]) + back[0] * (
        field - padded[:-2, 1:-1, 1:-1]
    )
    total = (
        total
        + trans[1] * (field - padded[1:-1, 2:, 1:-1])
        + back[1] * (field - padded[1:-1, :-2, 1:-1])
    )
    total = (
        total
        + trans[2] * (field - padded[1:-1, 1:-1, 2:])
        + back[2] * (field - padded[1:-1, 1:-1, :-2])
    )
    return total


def coarse_step(coarse, rhs_total, coefs, padded):
    dsum, plus_x, minus_x, plus_y, minus_y, plus_z, minus_z, cdiag = coefs
    applied = (
        dsum * coarse
        + plus_x * (coarse - padded[2:, 1:-1, 1:-1])
        + minus_x * (coarse - padded[:-2, 1:-1, 1:-1])
    )
    applied = (
        applied
        + plus_y * (coarse - padded[1:-1, 2:, 1:-1])
        + minus_y * (coarse - padded[1:-1, :-2, 1:-1])
    )
    applied = (
        applied
        + plus_z * (coarse - padded[1:-1, 1:-1, 2:])
        + minus_z * (coarse - padded[1:-1, 1:-1, :-2])
    )
    return coarse + omega_coarse * (rhs_total - applied) / cdiag


def least_squares(beta, h11, h21, h12, h22, h32):
    r11 = jnp.sqrt(h11 * h11 + h21 * h21)
    cos_one = h11 / r11
    sin_one = h21 / r11
    g_first = cos_one * beta
    g_second = -sin_one * beta
    upper = cos_one * h12 + sin_one * h22
    lower = cos_one * h22 - sin_one * h12
    r22 = jnp.sqrt(lower * lower + h32 * h32)
    second = lower * g_second / (r22 * r22)
    first = (g_first - upper * second) / r11
    return (first, second)


def shards(residual_eq, diag_block, mobility, trans, perf_cell, perf_well, perf_index):
    size_x = lax.axis_size("gx")
    size_y = lax.axis_size("gy")
    size_z = lax.axis_size("gz")
    cx, cy, cz = trans.shape[1:]
    ix = lax.axis_index("gx")
    iy = lax.axis_index("gy")
    iz = lax.axis_index("gz")

    local_well = perf_well[:, 0] - (device_number() - 1) * WELL_DEV

    slot_of_well = local_well[:, None] == jnp.arange(2 * WELL_DEV, dtype=local_well.dtype)[None, :]

    def well_partials(values):
        return jnp.sum(jnp.where(slot_of_well, values[:, None], 0.0), axis=0)

    def per_slot(table):
        return jnp.sum(jnp.where(slot_of_well, table[None, :], 0.0), axis=1)

    def exchange(field, partial):
        x_next = send_down(field[:1], "gx")
        x_prev = send_up(field[-1:], "gx")
        y_next = send_down(field[:, :1], "gy")
        y_prev = send_up(field[:, -1:], "gy")
        down = jnp.concatenate([field[:, :, 0].reshape(-1), partial[:WELL_DEV]])
        up = jnp.concatenate([field[:, :, -1].reshape(-1), partial[WELL_DEV:]])
        from_next = send_down(down, "gz")
        from_prev = send_up(up, "gz")
        z_next = from_next[: cx * cy].reshape(cx, cy, 1)
        z_prev = from_prev[: cx * cy].reshape(cx, cy, 1)
        totals = partial + jnp.concatenate([from_prev[cx * cy :], from_next[cx * cy :]])
        return (x_next, x_prev, y_next, y_prev, z_next, z_prev), totals

    weight_part = well_partials(perf_index)
    faces_t, weights = exchange(trans[2], weight_part)
    layer_x = send_up(trans[0, -1:], "gx")
    layer_y = send_up(trans[1][:, -1:], "gy")
    layer_z = faces_t[5]
    back = jnp.stack(
        [
            jnp.concatenate([layer_x, trans[0, :-1]], 0),
            jnp.concatenate([layer_y, trans[1][:, :-1]], 1),
            jnp.concatenate([layer_z, trans[2][:, :, :-1]], 2),
        ]
    )

    def flux(field, faces):
        return face_flux(field, faces, trans, back)

    columns = cx * cy
    column_hot = (perf_cell // cz)[:, None] == jnp.arange(columns, dtype=perf_cell.dtype)[None, :]
    column_hot = column_hot.astype(jnp.float32)
    depth_hot = ((perf_cell % cz)[:, None] == jnp.arange(cz, dtype=perf_cell.dtype)[None, :]).astype(
        jnp.float32
    )
    exact = lax.Precision.HIGHEST

    def flux_wells(field):
        picked = jnp.dot(column_hot, field.reshape(columns, cz), precision=exact)
        values = jnp.sum(picked * depth_hot, axis=1)
        faces, totals = exchange(field, well_partials(perf_index * values))
        bottom = per_slot(totals / weights)
        terms = perf_index * (values - bottom)
        wells = jnp.einsum("kc,kz->cz", column_hot, terms[:, None] * depth_hot, precision=exact)
        return flux(field, faces) + wells.reshape(field.shape)

    def jacobian(vector):
        coupling = flux_wells(vector[0])
        return (
            diag_block[:, 0] * vector[0]
            + diag_block[:, 1] * vector[1]
            + diag_block[:, 2] * vector[2]
            + mobility * coupling[None]
        )

    dpress = diag_block[0, 0] + diag_block[1, 0] + diag_block[2, 0]
    lam = mobility[0] + mobility[1] + mobility[2]
    pdiag = dpress + lam * (trans[0] + back[0] + trans[1] + back[1] + trans[2] + back[2])
    dsum = jnp.sum(dpress)
    plus_x = jnp.sum(lam[-1] * trans[0, -1])
    minus_x = jnp.sum(lam[0] * back[0, 0])
    plus_y = jnp.sum(lam[:, -1] * trans[1][:, -1])
    minus_y = jnp.sum(lam[:, 0] * back[1][:, 0])
    plus_z = jnp.sum(lam[:, :, -1] * trans[2][:, :, -1])
    minus_z = jnp.sum(lam[:, :, 0] * back[2][:, :, 0])

    rhs = -residual_eq
    start = gather_all(
        jnp.stack(
            [
                jnp.sum(rhs * rhs),
                jnp.sum(rhs[0] + rhs[1] + rhs[2]),
                dsum,
                plus_x,
                minus_x,
                plus_y,
                minus_y,
                plus_z,
                minus_z,
            ]
        )
    )
    grid = (size_x, size_y, size_z)
    beta = jnp.sqrt(jnp.sum(start[:, 0]))
    coarse_coefs = [start[:, k].reshape(grid) for k in range(2, 9)]
    cdiag = coarse_coefs[0]
    for value in coarse_coefs[1:]:
        cdiag = cdiag + value
    coarse_coefs = tuple(coarse_coefs) + (cdiag,)

    def coarse_solve(rhs_total):
        coarse = jnp.zeros(grid, jnp.float32)
        for sweep in range(CSWEEPS):
            coarse = coarse_step(coarse, rhs_total, coarse_coefs, jnp.pad(coarse, 1))
        padded = jnp.pad(coarse, 1)

        def at(dx, dy, dz):
            return padded[ix + 1 + dx, iy + 1 + dy, iz + 1 + dz]

        faces = (
            jnp.broadcast_to(at(1, 0, 0), (1, cy, cz)),
            jnp.broadcast_to(at(-1, 0, 0), (1, cy, cz)),
            jnp.broadcast_to(at(0, 1, 0), (cx, 1, cz)),
            jnp.broadcast_to(at(0, -1, 0), (cx, 1, cz)),
            jnp.broadcast_to(at(0, 0, 1), (cx, cy, 1)),
            jnp.broadcast_to(at(0, 0, -1), (cx, cy, 1)),
        )
        return at(0, 0, 0), faces

    def precondition(vector, rhs_total):
        rpress = vector[0] + vector[1] + vector[2]
        own, faces = coarse_solve(rhs_total)
        press = jnp.broadcast_to(own, rpress.shape)
        for sweep in range(FSWEEPS):
            if sweep:
                faces, _ = exchange(press, jnp.zeros((2 * WELL_DEV,), jnp.float32))
            press = press + omega_fine * (rpress - (dpress * press + lam * flux(press, faces))) / pdiag
        coupling = flux_wells(press)
        applied = diag_block[:, 0] * press + mobility * coupling[None]
        correction = block_solve(diag_block, vector - applied)
        return jnp.concatenate([(correction[0] + press)[None], correction[1:]], 0)

    first_basis = rhs / beta
    first_dir = precondition(first_basis, start[:, 1].reshape(grid) / beta)
    work = jacobian(first_dir)
    second = gather_all(
        jnp.stack(
            [
                jnp.sum(first_basis * work),
                jnp.sum(work * work),
                jnp.sum(first_basis * first_basis),
                jnp.sum(work[0] + work[1] + work[2]),
            ]
        )
    )
    h11 = jnp.sum(second[:, 0])
    norm_v1 = jnp.sum(second[:, 2])
    h21 = jnp.sqrt(jnp.sum(second[:, 1]) - 2.0 * h11 * h11 + h11 * h11 * norm_v1)
    applied_dir = precondition(work, second[:, 3].reshape(grid))
    second_basis = (work - h11 * first_basis) / h21
    second_dir = (applied_dir - h11 * first_dir) / h21
    work = jacobian(second_dir)
    sums = allsum(
        jnp.stack(
            [
                jnp.sum(first_basis * work),
                jnp.sum(second_basis * work),
                jnp.sum(work * work),
                jnp.sum(second_basis * second_basis),
                jnp.sum(first_basis * second_basis),
            ]
        )
    )
    h12 = sums[0]
    h22 = sums[1]
    h32 = jnp.sqrt(
        sums[2]
        + h12 * h12 * norm_v1
        + h22 * h22 * sums[3]
        - 2.0 * h12 * h12
        - 2.0 * h22 * h22
        + 2.0 * h12 * h22 * sums[4]
    )
    first, second = least_squares(beta, h11, h21, h12, h22, h32)
    return first * first_dir + second * second_dir


def solution(mesh):
    in_specs = (
        P(None, "gx", "gy", "gz"),
        P(None, None, "gx", "gy", "gz"),
        P(None, "gx", "gy", "gz"),
        P(None, "gx", "gy", "gz"),
        P(("gx", "gy", "gz")),
        P(("gx", "gy", "gz"), None),
        P(("gx", "gy", "gz")),
    )
    out_specs = P(None, "gx", "gy", "gz")
    return jax.shard_map(shards, mesh=mesh, in_specs=in_specs, out_specs=out_specs, check_vma=False)
```

```python
import jax
import jax.numpy as jnp
from jax import lax
from jax.sharding import PartitionSpec as P

WELL_DEV = 20
CSWEEPS = 4
FSWEEPS = 6


omega_fine = 0.7
omega_coarse = 0.7

AXES = ("gx", "gy", "gz")


def send_up(block, axis):
    size = lax.axis_size(axis)
    moved = lax.ppermute(block, axis, [(i, (i + 1) % size) for i in range(size)])
    return jnp.where(lax.axis_index(axis) == 0, jnp.zeros_like(moved), moved)


def send_down(block, axis):
    size = lax.axis_size(axis)
    moved = lax.ppermute(block, axis, [(i, (i - 1) % size) for i in range(size)])
    return jnp.where(lax.axis_index(axis) == size - 1, jnp.zeros_like(moved), moved)


def allsum(value):
    for axis in reversed(AXES):
        size = lax.axis_size(axis)
        if size & (size - 1):
            value = lax.psum(value, axis)
            continue
        step = 1
        while step < size:
            value = value + lax.ppermute(value, axis, [(i, i ^ step) for i in range(size)])
            step *= 2
    return value


def device_number():
    return (lax.axis_index("gx") * lax.axis_size("gy") + lax.axis_index("gy")) * lax.axis_size(
        "gz"
    ) + lax.axis_index("gz")


def gather_all(local):
    count = lax.axis_size("gx") * lax.axis_size("gy") * lax.axis_size("gz")
    slots = jnp.zeros((count, local.shape[0]), local.dtype).at[device_number()].set(local)
    return allsum(slots)


def block_solve(blocks, rhs):
    matrix = [[blocks[i, j] for j in range(3)] for i in range(3)]

    def cofactor(i, j):
        return (
            matrix[(i + 1) % 3][(j + 1) % 3] * matrix[(i + 2) % 3][(j + 2) % 3]
            - matrix[(i + 1) % 3][(j + 2) % 3] * matrix[(i + 2) % 3][(j + 1) % 3]
        )

    cofs = [[cofactor(i, j) for j in range(3)] for i in range(3)]
    determinant = matrix[0][0] * cofs[0][0] + matrix[0][1] * cofs[0][1] + matrix[0][2] * cofs[0][2]
    return jnp.stack(
        [
            (cofs[0][j] * rhs[0] + cofs[1][j] * rhs[1] + cofs[2][j] * rhs[2]) / determinant
            for j in range(3)
        ]
    )


def face_flux(field, faces, trans, back):
    x_next, x_prev, y_next, y_prev, z_next, z_prev = faces
    padded = jnp.concatenate([x_prev, field, x_next], 0)
    rim_x = ((1, 1), (0, 0), (0, 0))
    padded = jnp.concatenate([jnp.pad(y_prev, rim_x), padded, jnp.pad(y_next, rim_x)], 1)
    rim_xy = ((1, 1), (1, 1), (0, 0))
    padded = jnp.concatenate([jnp.pad(z_prev, rim_xy), padded, jnp.pad(z_next, rim_xy)], 2)
    total = trans[0] * (field - padded[2:, 1:-1, 1:-1]) + back[0] * (
        field - padded[:-2, 1:-1, 1:-1]
    )
    total = (
        total
        + trans[1] * (field - padded[1:-1, 2:, 1:-1])
        + back[1] * (field - padded[1:-1, :-2, 1:-1])
    )
    total = (
        total
        + trans[2] * (field - padded[1:-1, 1:-1, 2:])
        + back[2] * (field - padded[1:-1, 1:-1, :-2])
    )
    return total


def coarse_step(coarse, rhs_total, coefs, padded):
    dsum, plus_x, minus_x, plus_y, minus_y, plus_z, minus_z, cdiag = coefs
    applied = (
        dsum * coarse
        + plus_x * (coarse - padded[2:, 1:-1, 1:-1])
        + minus_x * (coarse - padded[:-2, 1:-1, 1:-1])
    )
    applied = (
        applied
        + plus_y * (coarse - padded[1:-1, 2:, 1:-1])
        + minus_y * (coarse - padded[1:-1, :-2, 1:-1])
    )
    applied = (
        applied
        + plus_z * (coarse - padded[1:-1, 1:-1, 2:])
        + minus_z * (coarse - padded[1:-1, 1:-1, :-2])
    )
    return coarse + omega_coarse * (rhs_total - applied) / cdiag


def least_squares(beta, h11, h21, h12, h22, h32):
    r11 = jnp.sqrt(h11 * h11 + h21 * h21)
    cos_one = h11 / r11
    sin_one = h21 / r11
    g_first = cos_one * beta
    g_second = -sin_one * beta
    upper = cos_one * h12 + sin_one * h22
    lower = cos_one * h22 - sin_one * h12
    r22 = jnp.sqrt(lower * lower + h32 * h32)
    second = lower * g_second / (r22 * r22)
    first = (g_first - upper * second) / r11
    return (first, second)


def shards(residual_eq, diag_block, mobility, trans, perf_cell, perf_well, perf_index):
    size_x = lax.axis_size("gx")
    size_y = lax.axis_size("gy")
    size_z = lax.axis_size("gz")
    cx, cy, cz = trans.shape[1:]
    ix = lax.axis_index("gx")
    iy = lax.axis_index("gy")
    iz = lax.axis_index("gz")

    local_well = perf_well[:, 0] - (device_number() - 1) * WELL_DEV

    slot_of_well = local_well[:, None] == jnp.arange(2 * WELL_DEV, dtype=local_well.dtype)[None, :]

    def well_partials(values):
        return jnp.sum(jnp.where(slot_of_well, values[:, None], 0.0), axis=0)

    def per_slot(table):
        return jnp.sum(jnp.where(slot_of_well, table[None, :], 0.0), axis=1)

    def exchange(field, partial):
        x_next = send_down(field[:1], "gx")
        x_prev = send_up(field[-1:], "gx")
        y_next = send_down(field[:, 0], "gy")[:, None]
        y_prev = send_up(field[:, -1], "gy")[:, None]
        down = jnp.concatenate([field[:, :, 0].reshape(-1), partial[:WELL_DEV]])
        up = jnp.concatenate([field[:, :, -1].reshape(-1), partial[WELL_DEV:]])
        from_next = send_down(down, "gz")
        from_prev = send_up(up, "gz")
        z_next = from_next[: cx * cy].reshape(cx, cy, 1)
        z_prev = from_prev[: cx * cy].reshape(cx, cy, 1)
        totals = partial + jnp.concatenate([from_prev[cx * cy :], from_next[cx * cy :]])
        return (x_next, x_prev, y_next, y_prev, z_next, z_prev), totals

    weight_part = well_partials(perf_index)
    faces_t, weights = exchange(trans[2], weight_part)
    layer_x = send_up(trans[0, -1:], "gx")
    layer_y = send_up(trans[1][:, -1:], "gy")
    layer_z = faces_t[5]
    back = jnp.stack(
        [
            jnp.concatenate([layer_x, trans[0, :-1]], 0),
            jnp.concatenate([layer_y, trans[1][:, :-1]], 1),
            jnp.concatenate([layer_z, trans[2][:, :, :-1]], 2),
        ]
    )

    def flux(field, faces):
        return face_flux(field, faces, trans, back)

    def flux_wells(field):
        flat = field.reshape(-1)
        values = flat[perf_cell]
        faces, totals = exchange(field, well_partials(perf_index * values))
        bottom = per_slot(totals / weights)
        terms = perf_index * (values - bottom)
        wells = jnp.zeros_like(flat).at[perf_cell].add(terms).reshape(field.shape)
        return flux(field, faces) + wells

    def jacobian(vector):
        coupling = flux_wells(vector[0])
        return (
            diag_block[:, 0] * vector[0]
            + diag_block[:, 1] * vector[1]
            + diag_block[:, 2] * vector[2]
            + mobility * coupling[None]
        )

    dpress = diag_block[0, 0] + diag_block[1, 0] + diag_block[2, 0]
    lam = mobility[0] + mobility[1] + mobility[2]
    pdiag = dpress + lam * (trans[0] + back[0] + trans[1] + back[1] + trans[2] + back[2])
    dsum = jnp.sum(dpress)
    plus_x = jnp.sum(lam[-1] * trans[0, -1])
    minus_x = jnp.sum(lam[0] * back[0, 0])
    plus_y = jnp.sum(lam[:, -1] * trans[1][:, -1])
    minus_y = jnp.sum(lam[:, 0] * back[1][:, 0])
    plus_z = jnp.sum(lam[:, :, -1] * trans[2][:, :, -1])
    minus_z = jnp.sum(lam[:, :, 0] * back[2][:, :, 0])

    rhs = -residual_eq
    start = gather_all(
        jnp.stack(
            [
                jnp.sum(rhs * rhs),
                jnp.sum(rhs[0] + rhs[1] + rhs[2]),
                dsum,
                plus_x,
                minus_x,
                plus_y,
                minus_y,
                plus_z,
                minus_z,
            ]
        )
    )
    grid = (size_x, size_y, size_z)
    beta = jnp.sqrt(jnp.sum(start[:, 0]))
    coarse_coefs = [start[:, k].reshape(grid) for k in range(2, 9)]
    cdiag = coarse_coefs[0]
    for value in coarse_coefs[1:]:
        cdiag = cdiag + value
    coarse_coefs = tuple(coarse_coefs) + (cdiag,)

    def coarse_solve(rhs_total):
        coarse = jnp.zeros(grid, jnp.float32)
        for sweep in range(CSWEEPS):
            coarse = coarse_step(coarse, rhs_total, coarse_coefs, jnp.pad(coarse, 1))
        padded = jnp.pad(coarse, 1)

        def at(dx, dy, dz):
            return padded[ix + 1 + dx, iy + 1 + dy, iz + 1 + dz]

        faces = (
            jnp.broadcast_to(at(1, 0, 0), (1, cy, cz)),
            jnp.broadcast_to(at(-1, 0, 0), (1, cy, cz)),
            jnp.broadcast_to(at(0, 1, 0), (cx, 1, cz)),
            jnp.broadcast_to(at(0, -1, 0), (cx, 1, cz)),
            jnp.broadcast_to(at(0, 0, 1), (cx, cy, 1)),
            jnp.broadcast_to(at(0, 0, -1), (cx, cy, 1)),
        )
        return at(0, 0, 0), faces

    def precondition(vector, rhs_total):
        rpress = vector[0] + vector[1] + vector[2]
        own, faces = coarse_solve(rhs_total)
        press = jnp.broadcast_to(own, rpress.shape)
        for sweep in range(FSWEEPS):
            if sweep:
                faces, _ = exchange(press, jnp.zeros((2 * WELL_DEV,), jnp.float32))
            press = press + omega_fine * (rpress - (dpress * press + lam * flux(press, faces))) / pdiag
        coupling = flux_wells(press)
        applied = diag_block[:, 0] * press + mobility * coupling[None]
        correction = block_solve(diag_block, vector - applied)
        return jnp.concatenate([(correction[0] + press)[None], correction[1:]], 0)

    first_basis = rhs / beta
    first_dir = precondition(first_basis, start[:, 1].reshape(grid) / beta)
    work = jacobian(first_dir)
    second = gather_all(
        jnp.stack(
            [
                jnp.sum(first_basis * work),
                jnp.sum(work * work),
                jnp.sum(first_basis * first_basis),
                jnp.sum(work[0] + work[1] + work[2]),
            ]
        )
    )
    h11 = jnp.sum(second[:, 0])
    norm_v1 = jnp.sum(second[:, 2])
    h21 = jnp.sqrt(jnp.sum(second[:, 1]) - 2.0 * h11 * h11 + h11 * h11 * norm_v1)
    applied_dir = precondition(work, second[:, 3].reshape(grid))
    second_basis = (work - h11 * first_basis) / h21
    second_dir = (applied_dir - h11 * first_dir) / h21
    work = jacobian(second_dir)
    sums = allsum(
        jnp.stack(
            [
                jnp.sum(first_basis * work),
                jnp.sum(second_basis * work),
                jnp.sum(work * work),
                jnp.sum(second_basis * second_basis),
                jnp.sum(first_basis * second_basis),
            ]
        )
    )
    h12 = sums[0]
    h22 = sums[1]
    h32 = jnp.sqrt(
        sums[2]
        + h12 * h12 * norm_v1
        + h22 * h22 * sums[3]
        - 2.0 * h12 * h12
        - 2.0 * h22 * h22
        + 2.0 * h12 * h22 * sums[4]
    )
    first, second = least_squares(beta, h11, h21, h12, h22, h32)
    return first * first_dir + second * second_dir


def solution(mesh):
    in_specs = (
        P(None, "gx", "gy", "gz"),
        P(None, None, "gx", "gy", "gz"),
        P(None, "gx", "gy", "gz"),
        P(None, "gx", "gy", "gz"),
        P(("gx", "gy", "gz")),
        P(("gx", "gy", "gz"), None),
        P(("gx", "gy", "gz")),
    )
    out_specs = P(None, "gx", "gy", "gz")
    return jax.shard_map(shards, mesh=mesh, in_specs=in_specs, out_specs=out_specs, check_vma=False)
```

```python
import jax
import jax.numpy as jnp
from jax import lax
from jax.sharding import PartitionSpec as P

WELL_DEV = 20
CSWEEPS = 4
FSWEEPS = 6


omega_fine = 0.7
omega_coarse = 0.7

AXES = ("gx", "gy", "gz")


def send_up(block, axis):
    size = lax.axis_size(axis)
    moved = lax.ppermute(block, axis, [(i, (i + 1) % size) for i in range(size)])
    return jnp.where(lax.axis_index(axis) == 0, jnp.zeros_like(moved), moved)


def send_down(block, axis):
    size = lax.axis_size(axis)
    moved = lax.ppermute(block, axis, [(i, (i - 1) % size) for i in range(size)])
    return jnp.where(lax.axis_index(axis) == size - 1, jnp.zeros_like(moved), moved)


def allsum(value):
    for axis in reversed(AXES):
        size = lax.axis_size(axis)
        if size & (size - 1):
            value = lax.psum(value, axis)
            continue
        step = 1
        while step < size:
            value = value + lax.ppermute(value, axis, [(i, i ^ step) for i in range(size)])
            step *= 2
    return value


def device_number():
    return (lax.axis_index("gx") * lax.axis_size("gy") + lax.axis_index("gy")) * lax.axis_size(
        "gz"
    ) + lax.axis_index("gz")


def gather_all(local):
    count = lax.axis_size("gx") * lax.axis_size("gy") * lax.axis_size("gz")
    slots = jnp.zeros((count, local.shape[0]), local.dtype).at[device_number()].set(local)
    return allsum(slots)


def block_solve(blocks, rhs):
    matrix = [[blocks[i, j] for j in range(3)] for i in range(3)]

    def cofactor(i, j):
        return (
            matrix[(i + 1) % 3][(j + 1) % 3] * matrix[(i + 2) % 3][(j + 2) % 3]
            - matrix[(i + 1) % 3][(j + 2) % 3] * matrix[(i + 2) % 3][(j + 1) % 3]
        )

    cofs = [[cofactor(i, j) for j in range(3)] for i in range(3)]
    determinant = matrix[0][0] * cofs[0][0] + matrix[0][1] * cofs[0][1] + matrix[0][2] * cofs[0][2]
    return jnp.stack(
        [
            (cofs[0][j] * rhs[0] + cofs[1][j] * rhs[1] + cofs[2][j] * rhs[2]) / determinant
            for j in range(3)
        ]
    )


def face_flux(field, faces, trans, back):
    x_next, x_prev, y_next, y_prev, z_next, z_prev = faces
    padded = jnp.concatenate([x_prev, field, x_next], 0)
    rim_x = ((1, 1), (0, 0), (0, 0))
    padded = jnp.concatenate([jnp.pad(y_prev, rim_x), padded, jnp.pad(y_next, rim_x)], 1)
    rim_xy = ((1, 1), (1, 1), (0, 0))
    padded = jnp.concatenate([jnp.pad(z_prev, rim_xy), padded, jnp.pad(z_next, rim_xy)], 2)
    total = trans[0] * (field - padded[2:, 1:-1, 1:-1]) + back[0] * (
        field - padded[:-2, 1:-1, 1:-1]
    )
    total = (
        total
        + trans[1] * (field - padded[1:-1, 2:, 1:-1])
        + back[1] * (field - padded[1:-1, :-2, 1:-1])
    )
    total = (
        total
        + trans[2] * (field - padded[1:-1, 1:-1, 2:])
        + back[2] * (field - padded[1:-1, 1:-1, :-2])
    )
    return total


def coarse_step(coarse, rhs_total, coefs, padded):
    dsum, plus_x, minus_x, plus_y, minus_y, plus_z, minus_z, cdiag = coefs
    applied = (
        dsum * coarse
        + plus_x * (coarse - padded[2:, 1:-1, 1:-1])
        + minus_x * (coarse - padded[:-2, 1:-1, 1:-1])
    )
    applied = (
        applied
        + plus_y * (coarse - padded[1:-1, 2:, 1:-1])
        + minus_y * (coarse - padded[1:-1, :-2, 1:-1])
    )
    applied = (
        applied
        + plus_z * (coarse - padded[1:-1, 1:-1, 2:])
        + minus_z * (coarse - padded[1:-1, 1:-1, :-2])
    )
    return coarse + omega_coarse * (rhs_total - applied) / cdiag


def least_squares(beta, h11, h21, h12, h22, h32):
    r11 = jnp.sqrt(h11 * h11 + h21 * h21)
    cos_one = h11 / r11
    sin_one = h21 / r11
    g_first = cos_one * beta
    g_second = -sin_one * beta
    upper = cos_one * h12 + sin_one * h22
    lower = cos_one * h22 - sin_one * h12
    r22 = jnp.sqrt(lower * lower + h32 * h32)
    second = lower * g_second / (r22 * r22)
    first = (g_first - upper * second) / r11
    return (first, second)


def shards(residual_eq, diag_block, mobility, trans, perf_cell, perf_well, perf_index):
    size_x = lax.axis_size("gx")
    size_y = lax.axis_size("gy")
    size_z = lax.axis_size("gz")
    cx, cy, cz = trans.shape[1:]
    ix = lax.axis_index("gx")
    iy = lax.axis_index("gy")
    iz = lax.axis_index("gz")

    local_well = perf_well[:, 0] - (device_number() - 1) * WELL_DEV

    slot_of_well = local_well[:, None] == jnp.arange(2 * WELL_DEV, dtype=local_well.dtype)[None, :]

    def well_partials(values):
        return jnp.sum(jnp.where(slot_of_well, values[:, None], 0.0), axis=0)

    def per_slot(table):
        return jnp.sum(jnp.where(slot_of_well, table[None, :], 0.0), axis=1)

    def exchange(field, partial):
        x_next = send_down(field[:1], "gx")
        x_prev = send_up(field[-1:], "gx")
        y_next = send_down(field[:, :1], "gy")
        y_prev = send_up(field[:, -1:], "gy")
        down = jnp.concatenate([field[:, :, 0].reshape(-1), partial[:WELL_DEV]])
        up = jnp.concatenate([field[:, :, -1].reshape(-1), partial[WELL_DEV:]])
        from_next = send_down(down, "gz")
        from_prev = send_up(up, "gz")
        z_next = from_next[: cx * cy].reshape(cx, cy, 1)
        z_prev = from_prev[: cx * cy].reshape(cx, cy, 1)
        totals = partial + jnp.concatenate([from_prev[cx * cy :], from_next[cx * cy :]])
        return (x_next, x_prev, y_next, y_prev, z_next, z_prev), totals

    weight_part = well_partials(perf_index)
    faces_t, weights = exchange(trans[2], weight_part)
    layer_x = send_up(trans[0, -1:], "gx")
    layer_y = send_up(trans[1][:, -1:], "gy")
    layer_z = faces_t[5]
    back = jnp.stack(
        [
            jnp.concatenate([layer_x, trans[0, :-1]], 0),
            jnp.concatenate([layer_y, trans[1][:, :-1]], 1),
            jnp.concatenate([layer_z, trans[2][:, :, :-1]], 2),
        ]
    )

    def flux(field, faces):
        return face_flux(field, faces, trans, back)

    def flux_wells(field):
        flat = field.reshape(-1)
        values = flat[perf_cell]
        faces, totals = exchange(field, well_partials(perf_index * values))
        bottom = per_slot(totals / weights)
        terms = perf_index * (values - bottom)
        wells = jnp.zeros_like(flat).at[perf_cell].add(terms).reshape(field.shape)
        return flux(field, faces) + wells

    def jacobian(vector):
        coupling = flux_wells(vector[0])
        return (
            diag_block[:, 0] * vector[0]
            + diag_block[:, 1] * vector[1]
            + diag_block[:, 2] * vector[2]
            + mobility * coupling[None]
        )

    dpress = diag_block[0, 0] + diag_block[1, 0] + diag_block[2, 0]
    lam = mobility[0] + mobility[1] + mobility[2]
    pdiag = dpress + lam * (trans[0] + back[0] + trans[1] + back[1] + trans[2] + back[2])
    dsum = jnp.sum(dpress)
    plus_x = jnp.sum(lam[-1] * trans[0, -1])
    minus_x = jnp.sum(lam[0] * back[0, 0])
    plus_y = jnp.sum(lam[:, -1] * trans[1][:, -1])
    minus_y = jnp.sum(lam[:, 0] * back[1][:, 0])
    plus_z = jnp.sum(lam[:, :, -1] * trans[2][:, :, -1])
    minus_z = jnp.sum(lam[:, :, 0] * back[2][:, :, 0])

    rhs = -residual_eq
    start = gather_all(
        jnp.stack(
            [
                jnp.sum(rhs * rhs),
                jnp.sum(rhs[0] + rhs[1] + rhs[2]),
                dsum,
                plus_x,
                minus_x,
                plus_y,
                minus_y,
                plus_z,
                minus_z,
            ]
        )
    )
    grid = (size_x, size_y, size_z)
    beta = jnp.sqrt(jnp.sum(start[:, 0]))
    coarse_coefs = [start[:, k].reshape(grid) for k in range(2, 9)]
    cdiag = coarse_coefs[0]
    for value in coarse_coefs[1:]:
        cdiag = cdiag + value
    coarse_coefs = tuple(coarse_coefs) + (cdiag,)

    def coarse_solve(rhs_total):
        coarse = jnp.zeros(grid, jnp.float32)
        for sweep in range(CSWEEPS):
            coarse = coarse_step(coarse, rhs_total, coarse_coefs, jnp.pad(coarse, 1))
        padded = jnp.pad(coarse, 1)

        def at(dx, dy, dz):
            return padded[ix + 1 + dx, iy + 1 + dy, iz + 1 + dz]

        faces = (
            jnp.broadcast_to(at(1, 0, 0), (1, cy, cz)),
            jnp.broadcast_to(at(-1, 0, 0), (1, cy, cz)),
            jnp.broadcast_to(at(0, 1, 0), (cx, 1, cz)),
            jnp.broadcast_to(at(0, -1, 0), (cx, 1, cz)),
            jnp.broadcast_to(at(0, 0, 1), (cx, cy, 1)),
            jnp.broadcast_to(at(0, 0, -1), (cx, cy, 1)),
        )
        return at(0, 0, 0), faces

    def precondition(vector, rhs_total):
        rpress = vector[0] + vector[1] + vector[2]
        own, faces = coarse_solve(rhs_total)
        press = jnp.broadcast_to(own, rpress.shape)
        def sweep(press, faces):
            return press + omega_fine * (rpress - (dpress * press + lam * flux(press, faces))) / pdiag

        def later_sweep(_, press):
            faces, _ = exchange(press, jnp.zeros((2 * WELL_DEV,), jnp.float32))
            return sweep(press, faces)

        press = lax.fori_loop(1, FSWEEPS, later_sweep, sweep(press, faces))
        coupling = flux_wells(press)
        applied = diag_block[:, 0] * press + mobility * coupling[None]
        correction = block_solve(diag_block, vector - applied)
        return jnp.concatenate([(correction[0] + press)[None], correction[1:]], 0)

    first_basis = rhs / beta
    first_dir = precondition(first_basis, start[:, 1].reshape(grid) / beta)
    work = jacobian(first_dir)
    second = gather_all(
        jnp.stack(
            [
                jnp.sum(first_basis * work),
                jnp.sum(work * work),
                jnp.sum(first_basis * first_basis),
                jnp.sum(work[0] + work[1] + work[2]),
            ]
        )
    )
    h11 = jnp.sum(second[:, 0])
    norm_v1 = jnp.sum(second[:, 2])
    h21 = jnp.sqrt(jnp.sum(second[:, 1]) - 2.0 * h11 * h11 + h11 * h11 * norm_v1)
    applied_dir = precondition(work, second[:, 3].reshape(grid))
    second_basis = (work - h11 * first_basis) / h21
    second_dir = (applied_dir - h11 * first_dir) / h21
    work = jacobian(second_dir)
    sums = allsum(
        jnp.stack(
            [
                jnp.sum(first_basis * work),
                jnp.sum(second_basis * work),
                jnp.sum(work * work),
                jnp.sum(second_basis * second_basis),
                jnp.sum(first_basis * second_basis),
            ]
        )
    )
    h12 = sums[0]
    h22 = sums[1]
    h32 = jnp.sqrt(
        sums[2]
        + h12 * h12 * norm_v1
        + h22 * h22 * sums[3]
        - 2.0 * h12 * h12
        - 2.0 * h22 * h22
        + 2.0 * h12 * h22 * sums[4]
    )
    first, second = least_squares(beta, h11, h21, h12, h22, h32)
    return first * first_dir + second * second_dir


def solution(mesh):
    in_specs = (
        P(None, "gx", "gy", "gz"),
        P(None, None, "gx", "gy", "gz"),
        P(None, "gx", "gy", "gz"),
        P(None, "gx", "gy", "gz"),
        P(("gx", "gy", "gz")),
        P(("gx", "gy", "gz"), None),
        P(("gx", "gy", "gz")),
    )
    out_specs = P(None, "gx", "gy", "gz")
    return jax.shard_map(shards, mesh=mesh, in_specs=in_specs, out_specs=out_specs, check_vma=False)
```

```python
import jax
import jax.numpy as jnp
from jax import lax
from jax.sharding import PartitionSpec as P

WELL_DEV = 20
CSWEEPS = 4
FSWEEPS = 6


omega_fine = 0.7
omega_coarse = 0.7

AXES = ("gx", "gy", "gz")


def send_up(block, axis):
    size = lax.axis_size(axis)
    moved = lax.ppermute(block, axis, [(i, (i + 1) % size) for i in range(size)])
    return jnp.where(lax.axis_index(axis) == 0, jnp.zeros_like(moved), moved)


def send_down(block, axis):
    size = lax.axis_size(axis)
    moved = lax.ppermute(block, axis, [(i, (i - 1) % size) for i in range(size)])
    return jnp.where(lax.axis_index(axis) == size - 1, jnp.zeros_like(moved), moved)


def allsum(value):
    for axis in reversed(AXES):
        size = lax.axis_size(axis)
        if size & (size - 1):
            value = lax.psum(value, axis)
            continue
        step = 1
        while step < size:
            value = value + lax.ppermute(value, axis, [(i, i ^ step) for i in range(size)])
            step *= 2
    return value


def device_number():
    return (lax.axis_index("gx") * lax.axis_size("gy") + lax.axis_index("gy")) * lax.axis_size(
        "gz"
    ) + lax.axis_index("gz")


def gather_all(local):
    count = lax.axis_size("gx") * lax.axis_size("gy") * lax.axis_size("gz")
    slots = jnp.zeros((count, local.shape[0]), local.dtype).at[device_number()].set(local)
    return allsum(slots)


def block_solve(blocks, rhs):
    matrix = [[blocks[i, j] for j in range(3)] for i in range(3)]

    def cofactor(i, j):
        return (
            matrix[(i + 1) % 3][(j + 1) % 3] * matrix[(i + 2) % 3][(j + 2) % 3]
            - matrix[(i + 1) % 3][(j + 2) % 3] * matrix[(i + 2) % 3][(j + 1) % 3]
        )

    cofs = [[cofactor(i, j) for j in range(3)] for i in range(3)]
    determinant = matrix[0][0] * cofs[0][0] + matrix[0][1] * cofs[0][1] + matrix[0][2] * cofs[0][2]
    return jnp.stack(
        [
            (cofs[0][j] * rhs[0] + cofs[1][j] * rhs[1] + cofs[2][j] * rhs[2]) / determinant
            for j in range(3)
        ]
    )


def face_flux(field, faces, trans, back):
    x_next, x_prev, y_next, y_prev, z_next, z_prev = faces
    padded = jnp.concatenate([x_prev, field, x_next], 0)
    rim_x = ((1, 1), (0, 0), (0, 0))
    padded = jnp.concatenate([jnp.pad(y_prev, rim_x), padded, jnp.pad(y_next, rim_x)], 1)
    rim_xy = ((1, 1), (1, 1), (0, 0))
    padded = jnp.concatenate([jnp.pad(z_prev, rim_xy), padded, jnp.pad(z_next, rim_xy)], 2)
    total = trans[0] * (field - padded[2:, 1:-1, 1:-1]) + back[0] * (
        field - padded[:-2, 1:-1, 1:-1]
    )
    total = (
        total
        + trans[1] * (field - padded[1:-1, 2:, 1:-1])
        + back[1] * (field - padded[1:-1, :-2, 1:-1])
    )
    total = (
        total
        + trans[2] * (field - padded[1:-1, 1:-1, 2:])
        + back[2] * (field - padded[1:-1, 1:-1, :-2])
    )
    return total


def coarse_step(coarse, rhs_total, coefs, padded):
    dsum, plus_x, minus_x, plus_y, minus_y, plus_z, minus_z, cdiag = coefs
    applied = (
        dsum * coarse
        + plus_x * (coarse - padded[2:, 1:-1, 1:-1])
        + minus_x * (coarse - padded[:-2, 1:-1, 1:-1])
    )
    applied = (
        applied
        + plus_y * (coarse - padded[1:-1, 2:, 1:-1])
        + minus_y * (coarse - padded[1:-1, :-2, 1:-1])
    )
    applied = (
        applied
        + plus_z * (coarse - padded[1:-1, 1:-1, 2:])
        + minus_z * (coarse - padded[1:-1, 1:-1, :-2])
    )
    return coarse + omega_coarse * (rhs_total - applied) / cdiag


def least_squares(beta, h11, h21, h12, h22, h32):
    r11 = jnp.sqrt(h11 * h11 + h21 * h21)
    cos_one = h11 / r11
    sin_one = h21 / r11
    g_first = cos_one * beta
    g_second = -sin_one * beta
    upper = cos_one * h12 + sin_one * h22
    lower = cos_one * h22 - sin_one * h12
    r22 = jnp.sqrt(lower * lower + h32 * h32)
    second = lower * g_second / (r22 * r22)
    first = (g_first - upper * second) / r11
    return (first, second)


def shards(residual_eq, diag_block, mobility, trans, perf_cell, perf_well, perf_index):
    size_x = lax.axis_size("gx")
    size_y = lax.axis_size("gy")
    size_z = lax.axis_size("gz")
    cx, cy, cz = trans.shape[1:]
    ix = lax.axis_index("gx")
    iy = lax.axis_index("gy")
    iz = lax.axis_index("gz")

    local_well = perf_well[:, 0] - (device_number() - 1) * WELL_DEV

    slot_of_well = local_well[:, None] == jnp.arange(2 * WELL_DEV, dtype=local_well.dtype)[None, :]

    def well_partials(values):
        return jnp.sum(jnp.where(slot_of_well, values[:, None], 0.0), axis=0)

    def per_slot(table):
        return jnp.sum(jnp.where(slot_of_well, table[None, :], 0.0), axis=1)

    def exchange(field, partial):
        x_next = send_down(field[:1], "gx")
        x_prev = send_up(field[-1:], "gx")
        y_next = send_down(field[:, :1], "gy")
        y_prev = send_up(field[:, -1:], "gy")
        down = field[:, :, 0].reshape(-1)
        up = field[:, :, -1].reshape(-1)
        if partial is not None:
            down = jnp.concatenate([down, partial[:WELL_DEV]])
            up = jnp.concatenate([up, partial[WELL_DEV:]])
        from_next = send_down(down, "gz")
        from_prev = send_up(up, "gz")
        z_next = from_next[: cx * cy].reshape(cx, cy, 1)
        z_prev = from_prev[: cx * cy].reshape(cx, cy, 1)
        if partial is None:
            return (x_next, x_prev, y_next, y_prev, z_next, z_prev), None
        totals = partial + jnp.concatenate([from_prev[cx * cy :], from_next[cx * cy :]])
        return (x_next, x_prev, y_next, y_prev, z_next, z_prev), totals

    weight_part = well_partials(perf_index)
    faces_t, weights = exchange(trans[2], weight_part)
    layer_x = send_up(trans[0, -1:], "gx")
    layer_y = send_up(trans[1][:, -1:], "gy")
    layer_z = faces_t[5]
    back = jnp.stack(
        [
            jnp.concatenate([layer_x, trans[0, :-1]], 0),
            jnp.concatenate([layer_y, trans[1][:, :-1]], 1),
            jnp.concatenate([layer_z, trans[2][:, :, :-1]], 2),
        ]
    )

    def flux(field, faces):
        return face_flux(field, faces, trans, back)

    def flux_wells(field):
        flat = field.reshape(-1)
        values = flat[perf_cell]
        faces, totals = exchange(field, well_partials(perf_index * values))
        bottom = per_slot(totals / weights)
        terms = perf_index * (values - bottom)
        wells = jnp.zeros_like(flat).at[perf_cell].add(terms).reshape(field.shape)
        return flux(field, faces) + wells

    def jacobian(vector):
        coupling = flux_wells(vector[0])
        return (
            diag_block[:, 0] * vector[0]
            + diag_block[:, 1] * vector[1]
            + diag_block[:, 2] * vector[2]
            + mobility * coupling[None]
        )

    dpress = diag_block[0, 0] + diag_block[1, 0] + diag_block[2, 0]
    lam = mobility[0] + mobility[1] + mobility[2]
    pdiag = dpress + lam * (trans[0] + back[0] + trans[1] + back[1] + trans[2] + back[2])
    dsum = jnp.sum(dpress)
    plus_x = jnp.sum(lam[-1] * trans[0, -1])
    minus_x = jnp.sum(lam[0] * back[0, 0])
    plus_y = jnp.sum(lam[:, -1] * trans[1][:, -1])
    minus_y = jnp.sum(lam[:, 0] * back[1][:, 0])
    plus_z = jnp.sum(lam[:, :, -1] * trans[2][:, :, -1])
    minus_z = jnp.sum(lam[:, :, 0] * back[2][:, :, 0])

    rhs = -residual_eq
    start = gather_all(
        jnp.stack(
            [
                jnp.sum(rhs * rhs),
                jnp.sum(rhs[0] + rhs[1] + rhs[2]),
                dsum,
                plus_x,
                minus_x,
                plus_y,
                minus_y,
                plus_z,
                minus_z,
            ]
        )
    )
    grid = (size_x, size_y, size_z)
    beta = jnp.sqrt(jnp.sum(start[:, 0]))
    coarse_coefs = [start[:, k].reshape(grid) for k in range(2, 9)]
    cdiag = coarse_coefs[0]
    for value in coarse_coefs[1:]:
        cdiag = cdiag + value
    coarse_coefs = tuple(coarse_coefs) + (cdiag,)

    def coarse_solve(rhs_total):
        coarse = jnp.zeros(grid, jnp.float32)
        for sweep in range(CSWEEPS):
            coarse = coarse_step(coarse, rhs_total, coarse_coefs, jnp.pad(coarse, 1))
        padded = jnp.pad(coarse, 1)

        def at(dx, dy, dz):
            return padded[ix + 1 + dx, iy + 1 + dy, iz + 1 + dz]

        faces = (
            jnp.broadcast_to(at(1, 0, 0), (1, cy, cz)),
            jnp.broadcast_to(at(-1, 0, 0), (1, cy, cz)),
            jnp.broadcast_to(at(0, 1, 0), (cx, 1, cz)),
            jnp.broadcast_to(at(0, -1, 0), (cx, 1, cz)),
            jnp.broadcast_to(at(0, 0, 1), (cx, cy, 1)),
            jnp.broadcast_to(at(0, 0, -1), (cx, cy, 1)),
        )
        return at(0, 0, 0), faces

    def precondition(vector, rhs_total):
        rpress = vector[0] + vector[1] + vector[2]
        own, faces = coarse_solve(rhs_total)
        press = jnp.broadcast_to(own, rpress.shape)
        for sweep in range(FSWEEPS):
            if sweep:
                faces, _ = exchange(press, None)
            press = press + omega_fine * (rpress - (dpress * press + lam * flux(press, faces))) / pdiag
        coupling = flux_wells(press)
        applied = diag_block[:, 0] * press + mobility * coupling[None]
        correction = block_solve(diag_block, vector - applied)
        return jnp.concatenate([(correction[0] + press)[None], correction[1:]], 0)

    first_basis = rhs / beta
    first_dir = precondition(first_basis, start[:, 1].reshape(grid) / beta)
    work = jacobian(first_dir)
    second = gather_all(
        jnp.stack(
            [
                jnp.sum(first_basis * work),
                jnp.sum(work * work),
                jnp.sum(first_basis * first_basis),
                jnp.sum(work[0] + work[1] + work[2]),
            ]
        )
    )
    h11 = jnp.sum(second[:, 0])
    norm_v1 = jnp.sum(second[:, 2])
    h21 = jnp.sqrt(jnp.sum(second[:, 1]) - 2.0 * h11 * h11 + h11 * h11 * norm_v1)
    applied_dir = precondition(work, second[:, 3].reshape(grid))
    second_basis = (work - h11 * first_basis) / h21
    second_dir = (applied_dir - h11 * first_dir) / h21
    work = jacobian(second_dir)
    sums = allsum(
        jnp.stack(
            [
                jnp.sum(first_basis * work),
                jnp.sum(second_basis * work),
                jnp.sum(work * work),
                jnp.sum(second_basis * second_basis),
                jnp.sum(first_basis * second_basis),
            ]
        )
    )
    h12 = sums[0]
    h22 = sums[1]
    h32 = jnp.sqrt(
        sums[2]
        + h12 * h12 * norm_v1
        + h22 * h22 * sums[3]
        - 2.0 * h12 * h12
        - 2.0 * h22 * h22
        + 2.0 * h12 * h22 * sums[4]
    )
    first, second = least_squares(beta, h11, h21, h12, h22, h32)
    return first * first_dir + second * second_dir


def solution(mesh):
    in_specs = (
        P(None, "gx", "gy", "gz"),
        P(None, None, "gx", "gy", "gz"),
        P(None, "gx", "gy", "gz"),
        P(None, "gx", "gy", "gz"),
        P(("gx", "gy", "gz")),
        P(("gx", "gy", "gz"), None),
        P(("gx", "gy", "gz")),
    )
    out_specs = P(None, "gx", "gy", "gz")
    return jax.shard_map(shards, mesh=mesh, in_specs=in_specs, out_specs=out_specs, check_vma=False)
```

```python
import jax
import jax.numpy as jnp
from jax import lax
from jax.sharding import PartitionSpec as P

WELL_DEV = 20
CSWEEPS = 4
FSWEEPS = 6


omega_fine = 0.7
omega_coarse = 0.7

AXES = ("gx", "gy", "gz")


def send_up(block, axis, zero_first=True):
    size = lax.axis_size(axis)
    moved = lax.ppermute(block, axis, [(i, (i + 1) % size) for i in range(size)])
    if not zero_first:
        return moved
    return jnp.where(lax.axis_index(axis) == 0, jnp.zeros_like(moved), moved)


def send_down(block, axis):
    size = lax.axis_size(axis)
    moved = lax.ppermute(block, axis, [(i, (i - 1) % size) for i in range(size)])
    return jnp.where(lax.axis_index(axis) == size - 1, jnp.zeros_like(moved), moved)


def allsum(value):
    for axis in reversed(AXES):
        size = lax.axis_size(axis)
        if size & (size - 1):
            value = lax.psum(value, axis)
            continue
        step = 1
        while step < size:
            value = value + lax.ppermute(value, axis, [(i, i ^ step) for i in range(size)])
            step *= 2
    return value


def device_number():
    return (lax.axis_index("gx") * lax.axis_size("gy") + lax.axis_index("gy")) * lax.axis_size(
        "gz"
    ) + lax.axis_index("gz")


def gather_all(local):
    count = lax.axis_size("gx") * lax.axis_size("gy") * lax.axis_size("gz")
    slots = jnp.zeros((count, local.shape[0]), local.dtype).at[device_number()].set(local)
    return allsum(slots)


def block_solve(blocks, rhs):
    matrix = [[blocks[i, j] for j in range(3)] for i in range(3)]

    def cofactor(i, j):
        return (
            matrix[(i + 1) % 3][(j + 1) % 3] * matrix[(i + 2) % 3][(j + 2) % 3]
            - matrix[(i + 1) % 3][(j + 2) % 3] * matrix[(i + 2) % 3][(j + 1) % 3]
        )

    cofs = [[cofactor(i, j) for j in range(3)] for i in range(3)]
    determinant = matrix[0][0] * cofs[0][0] + matrix[0][1] * cofs[0][1] + matrix[0][2] * cofs[0][2]
    return jnp.stack(
        [
            (cofs[0][j] * rhs[0] + cofs[1][j] * rhs[1] + cofs[2][j] * rhs[2]) / determinant
            for j in range(3)
        ]
    )


def face_flux(field, faces, trans, back):
    x_next, x_prev, y_next, y_prev, z_next, z_prev = faces
    padded = jnp.concatenate([x_prev, field, x_next], 0)
    rim_x = ((1, 1), (0, 0), (0, 0))
    padded = jnp.concatenate([jnp.pad(y_prev, rim_x), padded, jnp.pad(y_next, rim_x)], 1)
    rim_xy = ((1, 1), (1, 1), (0, 0))
    padded = jnp.concatenate([jnp.pad(z_prev, rim_xy), padded, jnp.pad(z_next, rim_xy)], 2)
    total = trans[0] * (field - padded[2:, 1:-1, 1:-1]) + back[0] * (
        field - padded[:-2, 1:-1, 1:-1]
    )
    total = (
        total
        + trans[1] * (field - padded[1:-1, 2:, 1:-1])
        + back[1] * (field - padded[1:-1, :-2, 1:-1])
    )
    total = (
        total
        + trans[2] * (field - padded[1:-1, 1:-1, 2:])
        + back[2] * (field - padded[1:-1, 1:-1, :-2])
    )
    return total


def coarse_step(coarse, rhs_total, coefs, padded):
    dsum, plus_x, minus_x, plus_y, minus_y, plus_z, minus_z, cdiag = coefs
    applied = (
        dsum * coarse
        + plus_x * (coarse - padded[2:, 1:-1, 1:-1])
        + minus_x * (coarse - padded[:-2, 1:-1, 1:-1])
    )
    applied = (
        applied
        + plus_y * (coarse - padded[1:-1, 2:, 1:-1])
        + minus_y * (coarse - padded[1:-1, :-2, 1:-1])
    )
    applied = (
        applied
        + plus_z * (coarse - padded[1:-1, 1:-1, 2:])
        + minus_z * (coarse - padded[1:-1, 1:-1, :-2])
    )
    return coarse + omega_coarse * (rhs_total - applied) / cdiag


def least_squares(beta, h11, h21, h12, h22, h32):
    r11 = jnp.sqrt(h11 * h11 + h21 * h21)
    cos_one = h11 / r11
    sin_one = h21 / r11
    g_first = cos_one * beta
    g_second = -sin_one * beta
    upper = cos_one * h12 + sin_one * h22
    lower = cos_one * h22 - sin_one * h12
    r22 = jnp.sqrt(lower * lower + h32 * h32)
    second = lower * g_second / (r22 * r22)
    first = (g_first - upper * second) / r11
    return (first, second)


def shards(residual_eq, diag_block, mobility, trans, perf_cell, perf_well, perf_index):
    size_x = lax.axis_size("gx")
    size_y = lax.axis_size("gy")
    size_z = lax.axis_size("gz")
    cx, cy, cz = trans.shape[1:]
    ix = lax.axis_index("gx")
    iy = lax.axis_index("gy")
    iz = lax.axis_index("gz")

    local_well = perf_well[:, 0] - (device_number() - 1) * WELL_DEV

    slot_of_well = local_well[:, None] == jnp.arange(2 * WELL_DEV, dtype=local_well.dtype)[None, :]

    def well_partials(values):
        return jnp.sum(jnp.where(slot_of_well, values[:, None], 0.0), axis=0)

    def per_slot(table):
        return jnp.sum(jnp.where(slot_of_well, table[None, :], 0.0), axis=1)

    def exchange(field, partial, zero_first=False):
        x_next = send_down(field[:1], "gx")
        x_prev = send_up(field[-1:], "gx", zero_first)
        y_next = send_down(field[:, :1], "gy")
        y_prev = send_up(field[:, -1:], "gy", zero_first)
        down = field[:, :, 0].reshape(-1)
        up = field[:, :, -1].reshape(-1)
        if partial is not None:
            down = jnp.concatenate([down, partial[:WELL_DEV]])
            up = jnp.concatenate([up, partial[WELL_DEV:]])
        from_next = send_down(down, "gz")
        from_prev = send_up(up, "gz", zero_first)
        z_next = from_next[: cx * cy].reshape(cx, cy, 1)
        z_prev = from_prev[: cx * cy].reshape(cx, cy, 1)
        if partial is None:
            return (x_next, x_prev, y_next, y_prev, z_next, z_prev), None
        totals = partial + jnp.concatenate([from_prev[cx * cy :], from_next[cx * cy :]])
        return (x_next, x_prev, y_next, y_prev, z_next, z_prev), totals

    weight_part = well_partials(perf_index)
    faces_t, weights = exchange(trans[2], weight_part, zero_first=True)
    layer_x = send_up(trans[0, -1:], "gx")
    layer_y = send_up(trans[1][:, -1:], "gy")
    layer_z = faces_t[5]
    back = jnp.stack(
        [
            jnp.concatenate([layer_x, trans[0, :-1]], 0),
            jnp.concatenate([layer_y, trans[1][:, :-1]], 1),
            jnp.concatenate([layer_z, trans[2][:, :, :-1]], 2),
        ]
    )

    def flux(field, faces):
        return face_flux(field, faces, trans, back)

    def flux_wells(field):
        flat = field.reshape(-1)
        values = flat[perf_cell]
        faces, totals = exchange(field, well_partials(perf_index * values))
        bottom = per_slot(totals / weights)
        terms = perf_index * (values - bottom)
        wells = jnp.zeros_like(flat).at[perf_cell].add(terms).reshape(field.shape)
        return flux(field, faces) + wells

    def jacobian(vector):
        coupling = flux_wells(vector[0])
        return (
            diag_block[:, 0] * vector[0]
            + diag_block[:, 1] * vector[1]
            + diag_block[:, 2] * vector[2]
            + mobility * coupling[None]
        )

    dpress = diag_block[0, 0] + diag_block[1, 0] + diag_block[2, 0]
    lam = mobility[0] + mobility[1] + mobility[2]
    pdiag = dpress + lam * (trans[0] + back[0] + trans[1] + back[1] + trans[2] + back[2])
    dsum = jnp.sum(dpress)
    plus_x = jnp.sum(lam[-1] * trans[0, -1])
    minus_x = jnp.sum(lam[0] * back[0, 0])
    plus_y = jnp.sum(lam[:, -1] * trans[1][:, -1])
    minus_y = jnp.sum(lam[:, 0] * back[1][:, 0])
    plus_z = jnp.sum(lam[:, :, -1] * trans[2][:, :, -1])
    minus_z = jnp.sum(lam[:, :, 0] * back[2][:, :, 0])

    rhs = -residual_eq
    start = gather_all(
        jnp.stack(
            [
                jnp.sum(rhs * rhs),
                jnp.sum(rhs[0] + rhs[1] + rhs[2]),
                dsum,
                plus_x,
                minus_x,
                plus_y,
                minus_y,
                plus_z,
                minus_z,
            ]
        )
    )
    grid = (size_x, size_y, size_z)
    beta = jnp.sqrt(jnp.sum(start[:, 0]))
    coarse_coefs = [start[:, k].reshape(grid) for k in range(2, 9)]
    cdiag = coarse_coefs[0]
    for value in coarse_coefs[1:]:
        cdiag = cdiag + value
    coarse_coefs = tuple(coarse_coefs) + (cdiag,)

    def coarse_solve(rhs_total):
        coarse = jnp.zeros(grid, jnp.float32)
        for sweep in range(CSWEEPS):
            coarse = coarse_step(coarse, rhs_total, coarse_coefs, jnp.pad(coarse, 1))
        padded = jnp.pad(coarse, 1)

        def at(dx, dy, dz):
            return padded[ix + 1 + dx, iy + 1 + dy, iz + 1 + dz]

        faces = (
            jnp.broadcast_to(at(1, 0, 0), (1, cy, cz)),
            jnp.broadcast_to(at(-1, 0, 0), (1, cy, cz)),
            jnp.broadcast_to(at(0, 1, 0), (cx, 1, cz)),
            jnp.broadcast_to(at(0, -1, 0), (cx, 1, cz)),
            jnp.broadcast_to(at(0, 0, 1), (cx, cy, 1)),
            jnp.broadcast_to(at(0, 0, -1), (cx, cy, 1)),
        )
        return at(0, 0, 0), faces

    def precondition(vector, rhs_total):
        rpress = vector[0] + vector[1] + vector[2]
        own, faces = coarse_solve(rhs_total)
        press = jnp.broadcast_to(own, rpress.shape)
        for sweep in range(FSWEEPS):
            if sweep:
                faces, _ = exchange(press, None)
            press = press + omega_fine * (rpress - (dpress * press + lam * flux(press, faces))) / pdiag
        coupling = flux_wells(press)
        applied = diag_block[:, 0] * press + mobility * coupling[None]
        correction = block_solve(diag_block, vector - applied)
        return jnp.concatenate([(correction[0] + press)[None], correction[1:]], 0)

    first_basis = rhs / beta
    first_dir = precondition(first_basis, start[:, 1].reshape(grid) / beta)
    work = jacobian(first_dir)
    second = gather_all(
        jnp.stack(
            [
                jnp.sum(first_basis * work),
                jnp.sum(work * work),
                jnp.sum(first_basis * first_basis),
                jnp.sum(work[0] + work[1] + work[2]),
            ]
        )
    )
    h11 = jnp.sum(second[:, 0])
    norm_v1 = jnp.sum(second[:, 2])
    h21 = jnp.sqrt(jnp.sum(second[:, 1]) - 2.0 * h11 * h11 + h11 * h11 * norm_v1)
    applied_dir = precondition(work, second[:, 3].reshape(grid))
    second_basis = (work - h11 * first_basis) / h21
    second_dir = (applied_dir - h11 * first_dir) / h21
    work = jacobian(second_dir)
    sums = allsum(
        jnp.stack(
            [
                jnp.sum(first_basis * work),
                jnp.sum(second_basis * work),
                jnp.sum(work * work),
                jnp.sum(second_basis * second_basis),
                jnp.sum(first_basis * second_basis),
            ]
        )
    )
    h12 = sums[0]
    h22 = sums[1]
    h32 = jnp.sqrt(
        sums[2]
        + h12 * h12 * norm_v1
        + h22 * h22 * sums[3]
        - 2.0 * h12 * h12
        - 2.0 * h22 * h22
        + 2.0 * h12 * h22 * sums[4]
    )
    first, second = least_squares(beta, h11, h21, h12, h22, h32)
    return first * first_dir + second * second_dir


def solution(mesh):
    in_specs = (
        P(None, "gx", "gy", "gz"),
        P(None, None, "gx", "gy", "gz"),
        P(None, "gx", "gy", "gz"),
        P(None, "gx", "gy", "gz"),
        P(("gx", "gy", "gz")),
        P(("gx", "gy", "gz"), None),
        P(("gx", "gy", "gz")),
    )
    out_specs = P(None, "gx", "gy", "gz")
    return jax.shard_map(shards, mesh=mesh, in_specs=in_specs, out_specs=out_specs, check_vma=False)
```

```python
import jax
import jax.numpy as jnp
from jax import lax
from jax.sharding import PartitionSpec as P

WELL_DEV = 20
CSWEEPS = 4
FSWEEPS = 6


omega_fine = 0.7
omega_coarse = 0.7

AXES = ("gx", "gy", "gz")


def send_up(block, axis, zero_first=True):
    size = lax.axis_size(axis)
    if zero_first:
        block = jnp.where(lax.axis_index(axis) == size - 1, jnp.zeros_like(block), block)
    return lax.ppermute(block, axis, [(i, (i + 1) % size) for i in range(size)])


def send_down(block, axis):
    size = lax.axis_size(axis)
    block = jnp.where(lax.axis_index(axis) == 0, jnp.zeros_like(block), block)
    return lax.ppermute(block, axis, [(i, (i - 1) % size) for i in range(size)])


def allsum(value):
    for axis in reversed(AXES):
        size = lax.axis_size(axis)
        if size & (size - 1):
            value = lax.psum(value, axis)
            continue
        step = 1
        while step < size:
            value = value + lax.ppermute(value, axis, [(i, i ^ step) for i in range(size)])
            step *= 2
    return value


def device_number():
    return (lax.axis_index("gx") * lax.axis_size("gy") + lax.axis_index("gy")) * lax.axis_size(
        "gz"
    ) + lax.axis_index("gz")


def gather_all(local):
    count = lax.axis_size("gx") * lax.axis_size("gy") * lax.axis_size("gz")
    slots = jnp.zeros((count, local.shape[0]), local.dtype).at[device_number()].set(local)
    return allsum(slots)


def block_solve(blocks, rhs):
    matrix = [[blocks[i, j] for j in range(3)] for i in range(3)]

    def cofactor(i, j):
        return (
            matrix[(i + 1) % 3][(j + 1) % 3] * matrix[(i + 2) % 3][(j + 2) % 3]
            - matrix[(i + 1) % 3][(j + 2) % 3] * matrix[(i + 2) % 3][(j + 1) % 3]
        )

    cofs = [[cofactor(i, j) for j in range(3)] for i in range(3)]
    determinant = matrix[0][0] * cofs[0][0] + matrix[0][1] * cofs[0][1] + matrix[0][2] * cofs[0][2]
    return jnp.stack(
        [
            (cofs[0][j] * rhs[0] + cofs[1][j] * rhs[1] + cofs[2][j] * rhs[2]) / determinant
            for j in range(3)
        ]
    )


def face_flux(field, faces, trans, back):
    x_next, x_prev, y_next, y_prev, z_next, z_prev = faces
    padded = jnp.concatenate([x_prev, field, x_next], 0)
    rim_x = ((1, 1), (0, 0), (0, 0))
    padded = jnp.concatenate([jnp.pad(y_prev, rim_x), padded, jnp.pad(y_next, rim_x)], 1)
    rim_xy = ((1, 1), (1, 1), (0, 0))
    padded = jnp.concatenate([jnp.pad(z_prev, rim_xy), padded, jnp.pad(z_next, rim_xy)], 2)
    total = trans[0] * (field - padded[2:, 1:-1, 1:-1]) + back[0] * (
        field - padded[:-2, 1:-1, 1:-1]
    )
    total = (
        total
        + trans[1] * (field - padded[1:-1, 2:, 1:-1])
        + back[1] * (field - padded[1:-1, :-2, 1:-1])
    )
    total = (
        total
        + trans[2] * (field - padded[1:-1, 1:-1, 2:])
        + back[2] * (field - padded[1:-1, 1:-1, :-2])
    )
    return total


def coarse_step(coarse, rhs_total, coefs, padded):
    dsum, plus_x, minus_x, plus_y, minus_y, plus_z, minus_z, cdiag = coefs
    applied = (
        dsum * coarse
        + plus_x * (coarse - padded[2:, 1:-1, 1:-1])
        + minus_x * (coarse - padded[:-2, 1:-1, 1:-1])
    )
    applied = (
        applied
        + plus_y * (coarse - padded[1:-1, 2:, 1:-1])
        + minus_y * (coarse - padded[1:-1, :-2, 1:-1])
    )
    applied = (
        applied
        + plus_z * (coarse - padded[1:-1, 1:-1, 2:])
        + minus_z * (coarse - padded[1:-1, 1:-1, :-2])
    )
    return coarse + omega_coarse * (rhs_total - applied) / cdiag


def least_squares(beta, h11, h21, h12, h22, h32):
    r11 = jnp.sqrt(h11 * h11 + h21 * h21)
    cos_one = h11 / r11
    sin_one = h21 / r11
    g_first = cos_one * beta
    g_second = -sin_one * beta
    upper = cos_one * h12 + sin_one * h22
    lower = cos_one * h22 - sin_one * h12
    r22 = jnp.sqrt(lower * lower + h32 * h32)
    second = lower * g_second / (r22 * r22)
    first = (g_first - upper * second) / r11
    return (first, second)


def shards(residual_eq, diag_block, mobility, trans, perf_cell, perf_well, perf_index):
    size_x = lax.axis_size("gx")
    size_y = lax.axis_size("gy")
    size_z = lax.axis_size("gz")
    cx, cy, cz = trans.shape[1:]
    ix = lax.axis_index("gx")
    iy = lax.axis_index("gy")
    iz = lax.axis_index("gz")

    local_well = perf_well[:, 0] - (device_number() - 1) * WELL_DEV

    slot_of_well = local_well[:, None] == jnp.arange(2 * WELL_DEV, dtype=local_well.dtype)[None, :]

    def well_partials(values):
        return jnp.sum(jnp.where(slot_of_well, values[:, None], 0.0), axis=0)

    def per_slot(table):
        return jnp.sum(jnp.where(slot_of_well, table[None, :], 0.0), axis=1)

    def exchange(field, partial, zero_first=False):
        x_next = send_down(field[:1], "gx")
        x_prev = send_up(field[-1:], "gx", zero_first)
        y_next = send_down(field[:, :1], "gy")
        y_prev = send_up(field[:, -1:], "gy", zero_first)
        down = field[:, :, 0].reshape(-1)
        up = field[:, :, -1].reshape(-1)
        if partial is not None:
            down = jnp.concatenate([down, partial[:WELL_DEV]])
            up = jnp.concatenate([up, partial[WELL_DEV:]])
        from_next = send_down(down, "gz")
        from_prev = send_up(up, "gz", zero_first)
        z_next = from_next[: cx * cy].reshape(cx, cy, 1)
        z_prev = from_prev[: cx * cy].reshape(cx, cy, 1)
        if partial is None:
            return (x_next, x_prev, y_next, y_prev, z_next, z_prev), None
        totals = partial + jnp.concatenate([from_prev[cx * cy :], from_next[cx * cy :]])
        return (x_next, x_prev, y_next, y_prev, z_next, z_prev), totals

    weight_part = well_partials(perf_index)
    faces_t, weights = exchange(trans[2], weight_part, zero_first=True)
    layer_x = send_up(trans[0, -1:], "gx")
    layer_y = send_up(trans[1][:, -1:], "gy")
    layer_z = faces_t[5]
    back = jnp.stack(
        [
            jnp.concatenate([layer_x, trans[0, :-1]], 0),
            jnp.concatenate([layer_y, trans[1][:, :-1]], 1),
            jnp.concatenate([layer_z, trans[2][:, :, :-1]], 2),
        ]
    )

    def flux(field, faces):
        return face_flux(field, faces, trans, back)

    def flux_wells(field):
        flat = field.reshape(-1)
        values = flat[perf_cell]
        faces, totals = exchange(field, well_partials(perf_index * values))
        bottom = per_slot(totals / weights)
        terms = perf_index * (values - bottom)
        wells = jnp.zeros_like(flat).at[perf_cell].add(terms).reshape(field.shape)
        return flux(field, faces) + wells

    def jacobian(vector):
        coupling = flux_wells(vector[0])
        return (
            diag_block[:, 0] * vector[0]
            + diag_block[:, 1] * vector[1]
            + diag_block[:, 2] * vector[2]
            + mobility * coupling[None]
        )

    dpress = diag_block[0, 0] + diag_block[1, 0] + diag_block[2, 0]
    lam = mobility[0] + mobility[1] + mobility[2]
    pdiag = dpress + lam * (trans[0] + back[0] + trans[1] + back[1] + trans[2] + back[2])
    dsum = jnp.sum(dpress)
    plus_x = jnp.sum(lam[-1] * trans[0, -1])
    minus_x = jnp.sum(lam[0] * back[0, 0])
    plus_y = jnp.sum(lam[:, -1] * trans[1][:, -1])
    minus_y = jnp.sum(lam[:, 0] * back[1][:, 0])
    plus_z = jnp.sum(lam[:, :, -1] * trans[2][:, :, -1])
    minus_z = jnp.sum(lam[:, :, 0] * back[2][:, :, 0])

    rhs = -residual_eq
    start = gather_all(
        jnp.stack(
            [
                jnp.sum(rhs * rhs),
                jnp.sum(rhs[0] + rhs[1] + rhs[2]),
                dsum,
                plus_x,
                minus_x,
                plus_y,
                minus_y,
                plus_z,
                minus_z,
            ]
        )
    )
    grid = (size_x, size_y, size_z)
    beta = jnp.sqrt(jnp.sum(start[:, 0]))
    coarse_coefs = [start[:, k].reshape(grid) for k in range(2, 9)]
    cdiag = coarse_coefs[0]
    for value in coarse_coefs[1:]:
        cdiag = cdiag + value
    coarse_coefs = tuple(coarse_coefs) + (cdiag,)

    def coarse_solve(rhs_total):
        coarse = jnp.zeros(grid, jnp.float32)
        for sweep in range(CSWEEPS):
            coarse = coarse_step(coarse, rhs_total, coarse_coefs, jnp.pad(coarse, 1))
        padded = jnp.pad(coarse, 1)

        def at(dx, dy, dz):
            return padded[ix + 1 + dx, iy + 1 + dy, iz + 1 + dz]

        faces = (
            jnp.broadcast_to(at(1, 0, 0), (1, cy, cz)),
            jnp.broadcast_to(at(-1, 0, 0), (1, cy, cz)),
            jnp.broadcast_to(at(0, 1, 0), (cx, 1, cz)),
            jnp.broadcast_to(at(0, -1, 0), (cx, 1, cz)),
            jnp.broadcast_to(at(0, 0, 1), (cx, cy, 1)),
            jnp.broadcast_to(at(0, 0, -1), (cx, cy, 1)),
        )
        return at(0, 0, 0), faces

    def precondition(vector, rhs_total):
        rpress = vector[0] + vector[1] + vector[2]
        own, faces = coarse_solve(rhs_total)
        press = jnp.broadcast_to(own, rpress.shape)
        for sweep in range(FSWEEPS):
            if sweep:
                faces, _ = exchange(press, None)
            press = press + omega_fine * (rpress - (dpress * press + lam * flux(press, faces))) / pdiag
        coupling = flux_wells(press)
        applied = diag_block[:, 0] * press + mobility * coupling[None]
        correction = block_solve(diag_block, vector - applied)
        return jnp.concatenate([(correction[0] + press)[None], correction[1:]], 0)

    first_basis = rhs / beta
    first_dir = precondition(first_basis, start[:, 1].reshape(grid) / beta)
    work = jacobian(first_dir)
    second = gather_all(
        jnp.stack(
            [
                jnp.sum(first_basis * work),
                jnp.sum(work * work),
                jnp.sum(first_basis * first_basis),
                jnp.sum(work[0] + work[1] + work[2]),
            ]
        )
    )
    h11 = jnp.sum(second[:, 0])
    norm_v1 = jnp.sum(second[:, 2])
    h21 = jnp.sqrt(jnp.sum(second[:, 1]) - 2.0 * h11 * h11 + h11 * h11 * norm_v1)
    applied_dir = precondition(work, second[:, 3].reshape(grid))
    second_basis = (work - h11 * first_basis) / h21
    second_dir = (applied_dir - h11 * first_dir) / h21
    work = jacobian(second_dir)
    sums = allsum(
        jnp.stack(
            [
                jnp.sum(first_basis * work),
                jnp.sum(second_basis * work),
                jnp.sum(work * work),
                jnp.sum(second_basis * second_basis),
                jnp.sum(first_basis * second_basis),
            ]
        )
    )
    h12 = sums[0]
    h22 = sums[1]
    h32 = jnp.sqrt(
        sums[2]
        + h12 * h12 * norm_v1
        + h22 * h22 * sums[3]
        - 2.0 * h12 * h12
        - 2.0 * h22 * h22
        + 2.0 * h12 * h22 * sums[4]
    )
    first, second = least_squares(beta, h11, h21, h12, h22, h32)
    return first * first_dir + second * second_dir


def solution(mesh):
    in_specs = (
        P(None, "gx", "gy", "gz"),
        P(None, None, "gx", "gy", "gz"),
        P(None, "gx", "gy", "gz"),
        P(None, "gx", "gy", "gz"),
        P(("gx", "gy", "gz")),
        P(("gx", "gy", "gz"), None),
        P(("gx", "gy", "gz")),
    )
    out_specs = P(None, "gx", "gy", "gz")
    return jax.shard_map(shards, mesh=mesh, in_specs=in_specs, out_specs=out_specs, check_vma=False)
```

```python
import jax
import jax.numpy as jnp
from jax import lax
from jax.sharding import PartitionSpec as P

WELL_DEV = 20
CSWEEPS = 4
FSWEEPS = 6


omega_fine = 0.7
omega_coarse = 0.7

AXES = ("gx", "gy", "gz")


def send_up(block, axis, zero_first=True):
    size = lax.axis_size(axis)
    moved = lax.ppermute(block, axis, [(i, (i + 1) % size) for i in range(size)])
    if not zero_first:
        return moved
    return jnp.where(lax.axis_index(axis) == 0, jnp.zeros_like(moved), moved)


def send_down(block, axis, zero_last=True):
    size = lax.axis_size(axis)
    moved = lax.ppermute(block, axis, [(i, (i - 1) % size) for i in range(size)])
    if not zero_last:
        return moved
    return jnp.where(lax.axis_index(axis) == size - 1, jnp.zeros_like(moved), moved)


def allsum(value):
    for axis in reversed(AXES):
        size = lax.axis_size(axis)
        if size & (size - 1):
            value = lax.psum(value, axis)
            continue
        step = 1
        while step < size:
            value = value + lax.ppermute(value, axis, [(i, i ^ step) for i in range(size)])
            step *= 2
    return value


def device_number():
    return (lax.axis_index("gx") * lax.axis_size("gy") + lax.axis_index("gy")) * lax.axis_size(
        "gz"
    ) + lax.axis_index("gz")


def gather_all(local):
    count = lax.axis_size("gx") * lax.axis_size("gy") * lax.axis_size("gz")
    slots = jnp.zeros((count, local.shape[0]), local.dtype).at[device_number()].set(local)
    return allsum(slots)


def block_solve(blocks, rhs):
    matrix = [[blocks[i, j] for j in range(3)] for i in range(3)]

    def cofactor(i, j):
        return (
            matrix[(i + 1) % 3][(j + 1) % 3] * matrix[(i + 2) % 3][(j + 2) % 3]
            - matrix[(i + 1) % 3][(j + 2) % 3] * matrix[(i + 2) % 3][(j + 1) % 3]
        )

    cofs = [[cofactor(i, j) for j in range(3)] for i in range(3)]
    determinant = matrix[0][0] * cofs[0][0] + matrix[0][1] * cofs[0][1] + matrix[0][2] * cofs[0][2]
    return jnp.stack(
        [
            (cofs[0][j] * rhs[0] + cofs[1][j] * rhs[1] + cofs[2][j] * rhs[2]) / determinant
            for j in range(3)
        ]
    )


def face_flux(field, faces, trans, back):
    x_next, x_prev, y_next, y_prev, z_next, z_prev = faces
    padded = jnp.concatenate([x_prev, field, x_next], 0)
    rim_x = ((1, 1), (0, 0), (0, 0))
    padded = jnp.concatenate([jnp.pad(y_prev, rim_x), padded, jnp.pad(y_next, rim_x)], 1)
    rim_xy = ((1, 1), (1, 1), (0, 0))
    padded = jnp.concatenate([jnp.pad(z_prev, rim_xy), padded, jnp.pad(z_next, rim_xy)], 2)
    total = trans[0] * (field - padded[2:, 1:-1, 1:-1]) + back[0] * (
        field - padded[:-2, 1:-1, 1:-1]
    )
    total = (
        total
        + trans[1] * (field - padded[1:-1, 2:, 1:-1])
        + back[1] * (field - padded[1:-1, :-2, 1:-1])
    )
    total = (
        total
        + trans[2] * (field - padded[1:-1, 1:-1, 2:])
        + back[2] * (field - padded[1:-1, 1:-1, :-2])
    )
    return total


def coarse_step(coarse, rhs_total, coefs, padded):
    dsum, plus_x, minus_x, plus_y, minus_y, plus_z, minus_z, cdiag = coefs
    applied = (
        dsum * coarse
        + plus_x * (coarse - padded[2:, 1:-1, 1:-1])
        + minus_x * (coarse - padded[:-2, 1:-1, 1:-1])
    )
    applied = (
        applied
        + plus_y * (coarse - padded[1:-1, 2:, 1:-1])
        + minus_y * (coarse - padded[1:-1, :-2, 1:-1])
    )
    applied = (
        applied
        + plus_z * (coarse - padded[1:-1, 1:-1, 2:])
        + minus_z * (coarse - padded[1:-1, 1:-1, :-2])
    )
    return coarse + omega_coarse * (rhs_total - applied) / cdiag


def least_squares(beta, h11, h21, h12, h22, h32):
    r11 = jnp.sqrt(h11 * h11 + h21 * h21)
    cos_one = h11 / r11
    sin_one = h21 / r11
    g_first = cos_one * beta
    g_second = -sin_one * beta
    upper = cos_one * h12 + sin_one * h22
    lower = cos_one * h22 - sin_one * h12
    r22 = jnp.sqrt(lower * lower + h32 * h32)
    second = lower * g_second / (r22 * r22)
    first = (g_first - upper * second) / r11
    return (first, second)


def shards(residual_eq, diag_block, mobility, trans, perf_cell, perf_well, perf_index):
    size_x = lax.axis_size("gx")
    size_y = lax.axis_size("gy")
    size_z = lax.axis_size("gz")
    cx, cy, cz = trans.shape[1:]
    ix = lax.axis_index("gx")
    iy = lax.axis_index("gy")
    iz = lax.axis_index("gz")

    local_well = perf_well[:, 0] - (device_number() - 1) * WELL_DEV

    slot_of_well = local_well[:, None] == jnp.arange(2 * WELL_DEV, dtype=local_well.dtype)[None, :]

    def well_partials(values):
        return jnp.sum(jnp.where(slot_of_well, values[:, None], 0.0), axis=0)

    def per_slot(table):
        return jnp.sum(jnp.where(slot_of_well, table[None, :], 0.0), axis=1)

    def exchange(field, partial, zero_first=False):
        x_next = send_down(field[:1], "gx", zero_first)
        x_prev = send_up(field[-1:], "gx", zero_first)
        y_next = send_down(field[:, :1], "gy", zero_first)
        y_prev = send_up(field[:, -1:], "gy", zero_first)
        down = field[:, :, 0].reshape(-1)
        up = field[:, :, -1].reshape(-1)
        if partial is not None:
            down = jnp.concatenate([down, partial[:WELL_DEV]])
            up = jnp.concatenate([up, partial[WELL_DEV:]])
        from_next = send_down(down, "gz", zero_first)
        from_prev = send_up(up, "gz", zero_first)
        z_next = from_next[: cx * cy].reshape(cx, cy, 1)
        z_prev = from_prev[: cx * cy].reshape(cx, cy, 1)
        if partial is None:
            return (x_next, x_prev, y_next, y_prev, z_next, z_prev), None
        totals = partial + jnp.concatenate([from_prev[cx * cy :], from_next[cx * cy :]])
        return (x_next, x_prev, y_next, y_prev, z_next, z_prev), totals

    weight_part = well_partials(perf_index)
    faces_t, weights = exchange(trans[2], weight_part, zero_first=True)
    layer_x = send_up(trans[0, -1:], "gx")
    layer_y = send_up(trans[1][:, -1:], "gy")
    layer_z = faces_t[5]
    back = jnp.stack(
        [
            jnp.concatenate([layer_x, trans[0, :-1]], 0),
            jnp.concatenate([layer_y, trans[1][:, :-1]], 1),
            jnp.concatenate([layer_z, trans[2][:, :, :-1]], 2),
        ]
    )

    edge = jnp.zeros_like(trans[0])
    inner = []
    for dim, (index, size) in enumerate(((ix, size_x), (iy, size_y), (iz, size_z))):
        layer = (jnp.arange(trans.shape[1 + dim]) == trans.shape[1 + dim] - 1) & (index == size - 1)
        shape = [1, 1, 1]
        shape[dim] = trans.shape[1 + dim]
        layer = layer.reshape(shape)
        edge = edge + jnp.where(layer, trans[dim], 0.0)
        inner.append(jnp.where(layer, 0.0, trans[dim]))
    trans_inner = jnp.stack(inner)

    def flux(field, faces):
        return face_flux(field, faces, trans_inner, back) + edge * field

    def flux_wells(field):
        flat = field.reshape(-1)
        values = flat[perf_cell]
        faces, totals = exchange(field, well_partials(perf_index * values))
        bottom = per_slot(totals / weights)
        terms = perf_index * (values - bottom)
        wells = jnp.zeros_like(flat).at[perf_cell].add(terms).reshape(field.shape)
        return flux(field, faces) + wells

    def jacobian(vector):
        coupling = flux_wells(vector[0])
        return (
            diag_block[:, 0] * vector[0]
            + diag_block[:, 1] * vector[1]
            + diag_block[:, 2] * vector[2]
            + mobility * coupling[None]
        )

    dpress = diag_block[0, 0] + diag_block[1, 0] + diag_block[2, 0]
    lam = mobility[0] + mobility[1] + mobility[2]
    pdiag = dpress + lam * (trans[0] + back[0] + trans[1] + back[1] + trans[2] + back[2])
    dsum = jnp.sum(dpress)
    plus_x = jnp.sum(lam[-1] * trans[0, -1])
    minus_x = jnp.sum(lam[0] * back[0, 0])
    plus_y = jnp.sum(lam[:, -1] * trans[1][:, -1])
    minus_y = jnp.sum(lam[:, 0] * back[1][:, 0])
    plus_z = jnp.sum(lam[:, :, -1] * trans[2][:, :, -1])
    minus_z = jnp.sum(lam[:, :, 0] * back[2][:, :, 0])

    rhs = -residual_eq
    start = gather_all(
        jnp.stack(
            [
                jnp.sum(rhs * rhs),
                jnp.sum(rhs[0] + rhs[1] + rhs[2]),
                dsum,
                plus_x,
                minus_x,
                plus_y,
                minus_y,
                plus_z,
                minus_z,
            ]
        )
    )
    grid = (size_x, size_y, size_z)
    beta = jnp.sqrt(jnp.sum(start[:, 0]))
    coarse_coefs = [start[:, k].reshape(grid) for k in range(2, 9)]
    cdiag = coarse_coefs[0]
    for value in coarse_coefs[1:]:
        cdiag = cdiag + value
    coarse_coefs = tuple(coarse_coefs) + (cdiag,)

    def coarse_solve(rhs_total):
        coarse = jnp.zeros(grid, jnp.float32)
        for sweep in range(CSWEEPS):
            coarse = coarse_step(coarse, rhs_total, coarse_coefs, jnp.pad(coarse, 1))
        padded = jnp.pad(coarse, 1)

        def at(dx, dy, dz):
            return padded[ix + 1 + dx, iy + 1 + dy, iz + 1 + dz]

        faces = (
            jnp.broadcast_to(at(1, 0, 0), (1, cy, cz)),
            jnp.broadcast_to(at(-1, 0, 0), (1, cy, cz)),
            jnp.broadcast_to(at(0, 1, 0), (cx, 1, cz)),
            jnp.broadcast_to(at(0, -1, 0), (cx, 1, cz)),
            jnp.broadcast_to(at(0, 0, 1), (cx, cy, 1)),
            jnp.broadcast_to(at(0, 0, -1), (cx, cy, 1)),
        )
        return at(0, 0, 0), faces

    def precondition(vector, rhs_total):
        rpress = vector[0] + vector[1] + vector[2]
        own, faces = coarse_solve(rhs_total)
        press = jnp.broadcast_to(own, rpress.shape)
        for sweep in range(FSWEEPS):
            if sweep:
                faces, _ = exchange(press, None)
            press = press + omega_fine * (rpress - (dpress * press + lam * flux(press, faces))) / pdiag
        coupling = flux_wells(press)
        applied = diag_block[:, 0] * press + mobility * coupling[None]
        correction = block_solve(diag_block, vector - applied)
        return jnp.concatenate([(correction[0] + press)[None], correction[1:]], 0)

    first_basis = rhs / beta
    first_dir = precondition(first_basis, start[:, 1].reshape(grid) / beta)
    work = jacobian(first_dir)
    second = gather_all(
        jnp.stack(
            [
                jnp.sum(first_basis * work),
                jnp.sum(work * work),
                jnp.sum(first_basis * first_basis),
                jnp.sum(work[0] + work[1] + work[2]),
            ]
        )
    )
    h11 = jnp.sum(second[:, 0])
    norm_v1 = jnp.sum(second[:, 2])
    h21 = jnp.sqrt(jnp.sum(second[:, 1]) - 2.0 * h11 * h11 + h11 * h11 * norm_v1)
    applied_dir = precondition(work, second[:, 3].reshape(grid))
    second_basis = (work - h11 * first_basis) / h21
    second_dir = (applied_dir - h11 * first_dir) / h21
    work = jacobian(second_dir)
    sums = allsum(
        jnp.stack(
            [
                jnp.sum(first_basis * work),
                jnp.sum(second_basis * work),
                jnp.sum(work * work),
                jnp.sum(second_basis * second_basis),
                jnp.sum(first_basis * second_basis),
            ]
        )
    )
    h12 = sums[0]
    h22 = sums[1]
    h32 = jnp.sqrt(
        sums[2]
        + h12 * h12 * norm_v1
        + h22 * h22 * sums[3]
        - 2.0 * h12 * h12
        - 2.0 * h22 * h22
        + 2.0 * h12 * h22 * sums[4]
    )
    first, second = least_squares(beta, h11, h21, h12, h22, h32)
    return first * first_dir + second * second_dir


def solution(mesh):
    in_specs = (
        P(None, "gx", "gy", "gz"),
        P(None, None, "gx", "gy", "gz"),
        P(None, "gx", "gy", "gz"),
        P(None, "gx", "gy", "gz"),
        P(("gx", "gy", "gz")),
        P(("gx", "gy", "gz"), None),
        P(("gx", "gy", "gz")),
    )
    out_specs = P(None, "gx", "gy", "gz")
    return jax.shard_map(shards, mesh=mesh, in_specs=in_specs, out_specs=out_specs, check_vma=False)
```
